256 devices in a mesh: req: 32 (over z_hi, x, y), tp: 8 (over z_lo, core).
Axes of the slice: x: 4, y: 4, z: 8 (z_hi: 2, z_lo: 4; z = z_hi * 4 + z_lo), core: 2. Of those that a mesh axis runs over, the one named last changes fastest.
Arguments:
- tokens: bfloat16 [8192, 2560], P('req'), may hold values from -6 to 6
- norm_gain: float32 [2560], replicated, may hold values from 0.1 to 1.9
- w_query: bfloat16 [2560, 2560], P(None, 'tp')
- w_key: bfloat16 [2560, 640], P(None, 'tp')
- w_value: bfloat16 [2560, 640], P(None, 'tp'), may hold values from -0.125 to 0.125
- page_counts: int32 [16], replicated, may hold values from 1 to 128, 512 in all
- pad_counts: int32 [16], replicated, may hold values from 0 to 15
- page_table: int32 [32, 16], P('req'), may hold values from 0 to 15, each once within a row
Outputs:
- context: bfloat16 [8192, 2560], P('req', 'tp')
- cache: bfloat16 [512, 8, 2560], P(('req', 'tp'))
The draws below stay inside these ranges and needn't reach their ends.
Inputs may be any that keep to these rules, and one draw needn't show every extreme that they name: `page_counts`: each prompt has at least one live slot; the slots of all prompts fill the stream exactly. `page_table`: each row is a permutation; cache slot s of a block belongs to tp index s // 2.
All inputs are finite; a program needn't handle non-finite values.
Results may differ from the reference program's by a relative error of at most 0.012.
Values may be sent and summed in bfloat16 or wider, within the bound.
No kernel may reach another device: no remote copies, remote signals or barrier semaphores. Data moves between devices by JAX's collectives and lax.ppermute only.
A program may use at most 64 MiB of HBM per device.

```python
import math
import jax
import jax.numpy as jnp
import numpy as np
from jax import lax

D = 2560
HQ = 32
N_KVH = 8
HD = 80
WINDOW = 4096
PAGE = 16
TOK_DEV = 256
TOKENS = 8192
PPD = 16
NSEQ = 16
LONGEST = 2048
DEPTH = 8
N_REQ = 32


def key_weights(key):
    sub_key = jax.random.fold_in(key, 7177)
    values = jax.random.normal(sub_key, (D, N_KVH * HD), jnp.float32)
    return values * D ** (-0.5)


def draw_w_key(key, part):
    return key_weights(key).astype(jnp.bfloat16)


def draw_w_query(key, part):
    sub_key = jax.random.fold_in(key, 5113)
    spread = 2.4 * D ** (-0.5)
    values = jax.random.normal(sub_key, (D, HQ * HD), jnp.float32) * spread
    return values.astype(jnp.bfloat16)


def touch_ends(values, stream_key, least, top_value):
    index_at = [jax.random.randint(jax.random.fold_in(stream_key, axis), (), 0, length) for axis, length in enumerate(values.shape)]
    widest = values.shape.index(max(values.shape))
    neighbour = index_at[:widest] + [(index_at[widest] + 1) % values.shape[widest]] + index_at[widest + 1:]
    return values.at[tuple(index_at)].set(least).at[tuple(neighbour)].set(top_value)


def levels(own_key, dims, shards, low, top_value):
    def one(axis_at, blocks):
        draws = jax.random.uniform(jax.random.fold_in(jax.random.fold_in(own_key, 6), axis_at), (blocks,), jnp.float32, low / len(shards), top_value / len(shards))
        return jnp.repeat(jnp.exp(draws), dims[axis_at] // blocks).reshape((-1,) + (1,) * (len(dims) - axis_at - 1))

    level = one(*shards[0])
    for cut in shards[1:]:
        level = level * one(*cut)
    return level


def length_profile(count, total, limit, skew):
    weights = [(1 << 20) // math.isqrt(rank ** skew) + 1 for rank in range(2, count + 1)]
    surplus, given = total - limit - (count - 1), [1] * (count - 1)
    while surplus > 0:
        movable = [i for i in range(count - 1) if given[i] < limit]
        pool, budget = sum([weights[i] for i in movable]), surplus
        for i in movable:
            more = min(limit - given[i], max(1, budget * weights[i] // pool), surplus)
            given[i] = given[i] + more
            surplus = surplus - more
    return np.array([limit] + given)


def uneven(key, number_of, total, most, skew):
    if number_of == 2:
        one = jax.random.randint(key, (), max(1, total - most), min(most, total - 1) + 1)
        return jnp.stack([one, total - one])
    sizes = jnp.asarray(length_profile(number_of, total, most, skew), jnp.int32)
    pairs = (number_of - 1) // 2
    donor, taker = sizes[1:1 + 2 * pairs:2], sizes[2:2 + 2 * pairs:2]
    room = jnp.minimum(donor - 1, most - taker)
    moved = jax.random.randint(jax.random.fold_in(key, 1), (pairs,), 0, 1 << 20) % (room + 1)
    sizes = sizes.at[1:1 + 2 * pairs:2].set(donor - moved).at[2:2 + 2 * pairs:2].set(taker + moved)
    return sizes[jax.random.permutation(jax.random.fold_in(key, 2), number_of)]


def scatter_about(rng, shape, scale, bound, shards=(), held_as=jnp.bfloat16):
    array = scale * jax.random.normal(rng, shape, jnp.float32)
    if shards:
        array = array * levels(rng, shape, shards, -0.22, 0.18)
    return jnp.clip(array, -bound, bound).astype(held_as)


def setup_inputs(seed: int = 0) -> dict:
    key_list = jax.random.split(jax.random.key(seed), 9)
    tokens = scatter_about(key_list[0], (TOKENS, D), 1.0, 6.0, ((0, 32),))
    norm_gain = jnp.clip(1.0 + 0.18 * jax.random.normal(key_list[1], (D,), jnp.float32), 0.1, 1.9)
    w_query = draw_w_query(jax.random.fold_in(key_list[8], 71), 0)
    w_key = draw_w_key(jax.random.fold_in(key_list[8], 71), 0)
    w_value = scatter_about(key_list[4], (D, N_KVH * HD), D ** -0.5, 0.125, ((1, 8),))
    page_counts = uneven(key_list[5], NSEQ, TOKENS // PAGE, LONGEST // PAGE, 2).astype(jnp.int32)
    pad_counts = touch_ends(jax.random.randint(key_list[6], (NSEQ,), 0, PAGE), jax.random.fold_in(key_list[6], 1), 0, PAGE - 1).astype(jnp.int32)
    page_table = jax.vmap(lambda own: jax.random.permutation(own, PPD))(jax.random.split(key_list[7], N_REQ)).reshape((N_REQ, PPD)).astype(jnp.int32)
    return {"tokens": tokens, "norm_gain": norm_gain, "w_query": w_query, "w_key": w_key, "w_value": w_value, "page_counts": page_counts, "pad_counts": pad_counts, "page_table": page_table}


NORM_EPS = 1e-05
ROPE_BASE = 10000.0
MASKED_SCORE = -1e+30

def token_meta(slot_index, page_counts, pad_counts):
    prompt_count = page_counts.shape[0]
    slot_counts = page_counts * PAGE
    slot_ends = jnp.cumsum(slot_counts).astype(jnp.int32)
    segment_id = lax.optimization_barrier(jnp.sum((slot_index[:, None] >= slot_ends[None, :]).astype(jnp.int32), axis=1))
    one_hot = (segment_id[:, None] == jnp.arange(prompt_count, dtype=jnp.int32)[None, :]).astype(jnp.int32)
    first_slot = lax.optimization_barrier(jnp.sum(one_hot * (slot_ends - slot_counts)[None, :], axis=1))
    live_count = lax.optimization_barrier(jnp.sum(one_hot * (slot_counts - pad_counts)[None, :], axis=1))
    position = slot_index - first_slot
    inside = slot_index >= 0
    is_live = (position < live_count) & inside
    segment_id = jnp.where(inside, segment_id, -1)
    return (segment_id, position, is_live)

def rotate(vectors, position):
    half_width = vectors.shape[-1] // 2
    frequency = ROPE_BASE ** (-2.0 * jnp.arange(half_width, dtype=jnp.float32) / vectors.shape[-1])
    angles = position.astype(jnp.float32)[:, None, None] * frequency[None, None, :]
    cosine = jnp.cos(angles)
    sine_part = jnp.sin(angles)
    front_half = vectors[..., :half_width]
    back_half = vectors[..., half_width:]
    return jnp.concatenate([front_half * cosine - back_half * sine_part, back_half * cosine + front_half * sine_part], axis=-1)

def project(tokens, norm_gain, w_query, w_key, w_value, position):
    row_count = tokens.shape[0]
    as_float = tokens.astype(jnp.float32)
    normed = (as_float * lax.rsqrt(lax.optimization_barrier(jnp.mean(as_float * as_float, axis=-1, keepdims=True)) + NORM_EPS) * norm_gain).astype(jnp.bfloat16)
    query_rot = jnp.dot(normed, w_query, preferred_element_type=jnp.float32).reshape(row_count, -1, HD)
    query_rot = rotate(query_rot, position).astype(jnp.bfloat16)
    key_rot = jnp.dot(normed, w_key, preferred_element_type=jnp.float32).reshape(row_count, -1, HD)
    key_rot = rotate(key_rot, position).astype(jnp.bfloat16)
    value_rows = jnp.dot(normed, w_value, preferred_element_type=jnp.float32).reshape(row_count, -1, HD).astype(jnp.bfloat16)
    return (query_rot, key_rot, value_rows)

def reference(tokens, norm_gain, w_query, w_key, w_value, page_counts, pad_counts, page_table):
    slot_index = jnp.arange(TOKENS, dtype=jnp.int32)
    segment_id, position, is_live = token_meta(slot_index, page_counts, pad_counts)
    query_rot, key_rot, value_rows = project(tokens, norm_gain, w_query, w_key, w_value, position)
    group_size = HQ // N_KVH
    reach = DEPTH * TOK_DEV
    span = reach + TOK_DEV
    key_pad = jnp.concatenate([jnp.zeros((reach, N_KVH, HD), jnp.bfloat16), key_rot], axis=0)
    value_pad = jnp.concatenate([jnp.zeros((reach, N_KVH, HD), jnp.bfloat16), value_rows], axis=0)
    key_index = jnp.arange(TOKENS + reach, dtype=jnp.int32) - reach
    key_segment, unused_position, key_live = token_meta(key_index, page_counts, pad_counts)
    score_scale = HD ** (-0.5)

    def one_block(block_id):
        first = (block_id * TOK_DEV).astype(jnp.int32)
        queries = lax.dynamic_slice_in_dim(query_rot, first, TOK_DEV, 0).astype(jnp.float32).reshape(TOK_DEV, N_KVH, group_size, HD)
        keys_here = lax.dynamic_slice_in_dim(key_pad, first, span, 0).astype(jnp.float32)
        values_here = lax.dynamic_slice_in_dim(value_pad, first, span, 0).astype(jnp.float32)
        query_index = lax.dynamic_slice_in_dim(slot_index, first, TOK_DEV, 0)
        query_segment = lax.dynamic_slice_in_dim(segment_id, first, TOK_DEV, 0)
        query_live = lax.dynamic_slice_in_dim(is_live, first, TOK_DEV, 0)
        near_index = lax.dynamic_slice_in_dim(key_index, first, span, 0)
        near_segment = lax.dynamic_slice_in_dim(key_segment, first, span, 0)
        near_live = lax.dynamic_slice_in_dim(key_live, first, span, 0)
        allowed = (near_segment[None, :] == query_segment[:, None]) & near_live[None, :]
        allowed = allowed & (near_index[None, :] <= query_index[:, None]) & (query_index[:, None] - near_index[None, :] < WINDOW)

        def one_head(head_id):
            head_queries = lax.dynamic_index_in_dim(queries, head_id, 1, keepdims=False)
            head_keys = lax.dynamic_index_in_dim(keys_here, head_id, 1, keepdims=False)
            head_values = lax.dynamic_index_in_dim(values_here, head_id, 1, keepdims=False)
            scores = jnp.einsum('qjd,kd->jqk', head_queries, head_keys) * score_scale
            scores = jnp.where(allowed[None], scores, MASKED_SCORE)
            row_max = lax.optimization_barrier(jnp.max(scores, axis=-1, keepdims=True))
            probs = jnp.where(allowed[None], jnp.exp(scores - row_max), 0.0)
            prob_total = lax.optimization_barrier(jnp.sum(probs, axis=-1))
            weights = lax.optimization_barrier(probs.astype(jnp.bfloat16)).astype(jnp.float32)
            weighted = jnp.einsum('jqk,kd->jqd', weights, head_values)
            return weighted / prob_total[..., None]
        per_head = lax.map(one_head, jnp.arange(N_KVH, dtype=jnp.int32))
        result = jnp.transpose(per_head, (2, 0, 1, 3)).reshape(TOK_DEV, HQ * HD)
        result = jnp.where(query_live[:, None], result, 0.0)
        return result.astype(jnp.bfloat16)
    blocks = lax.map(one_block, jnp.arange(TOKENS // TOK_DEV, dtype=jnp.int32))
    context = blocks.reshape(TOKENS, HQ * HD)
    packed = jnp.concatenate([key_rot, value_rows], axis=-1)
    live_rows = jnp.where(is_live[:, None, None], packed, jnp.zeros((), jnp.bfloat16))
    page_rows = live_rows.reshape(TOKENS // PAGE, PAGE, N_KVH, 2 * HD).transpose(0, 2, 1, 3).reshape(TOKENS // PAGE, N_KVH, PAGE * 2 * HD)
    target = (jnp.arange(N_REQ, dtype=jnp.int32)[:, None] * PPD + page_table).reshape(-1)
    cache = jnp.zeros_like(page_rows).at[target].set(page_rows)
    return (context, cache)
```

```python
import jax
import jax.numpy as jnp
from jax import lax
from jax.sharding import PartitionSpec as P

HD = 80
WINDOW = 4096
PAGE = 16


NORM_EPS = 1e-05
ROPE_BASE = 10000.0
MASKED_SCORE = -1e30


def passed_along(x, axis, by):
    size = lax.axis_size(axis)
    pairs = [(i, i + by) for i in range(size) if 0 <= i + by < size]
    return lax.ppermute(x, axis, pairs)


def token_meta(slot_index, page_counts, pad_counts):
    prompt_count = page_counts.shape[0]
    slot_counts = page_counts * PAGE
    slot_ends = jnp.cumsum(slot_counts)
    segment_id = jnp.sum((slot_index[:, None] >= slot_ends[None, :]).astype(jnp.int32), axis=1)
    one_hot = (segment_id[:, None] == jnp.arange(prompt_count, dtype=jnp.int32)[None, :]).astype(
        jnp.int32
    )
    first_slot = jnp.sum(one_hot * (slot_ends - slot_counts)[None, :], axis=1)
    live_count = jnp.sum(one_hot * (slot_counts - pad_counts)[None, :], axis=1)
    position = slot_index - first_slot
    inside = slot_index >= 0
    is_live = (position < live_count) & inside
    segment_id = jnp.where(inside, segment_id, -1)
    return (segment_id, position, is_live)


def rotate(vectors, position):
    half_width = vectors.shape[-1] // 2
    frequency = ROPE_BASE ** (-2.0 * jnp.arange(half_width, dtype=jnp.float32) / vectors.shape[-1])
    angles = position.astype(jnp.float32)[:, None, None] * frequency[None, None, :]
    cosine = jnp.cos(angles)
    sine_part = jnp.sin(angles)
    front_half = vectors[..., :half_width]
    back_half = vectors[..., half_width:]
    return jnp.concatenate(
        [front_half * cosine - back_half * sine_part, back_half * cosine + front_half * sine_part],
        axis=-1,
    )


def project(tokens, norm_gain, w_query, w_key, w_value, position):
    row_count = tokens.shape[0]
    as_float = tokens.astype(jnp.float32)
    normed = (
        as_float
        * lax.rsqrt(jnp.mean(as_float * as_float, axis=-1, keepdims=True) + NORM_EPS)
        * norm_gain
    ).astype(jnp.bfloat16)
    query_rot = jnp.dot(normed, w_query, preferred_element_type=jnp.float32).reshape(
        row_count, -1, HD
    )
    query_rot = rotate(query_rot, position).astype(jnp.bfloat16)
    key_rot = jnp.dot(normed, w_key, preferred_element_type=jnp.float32).reshape(row_count, -1, HD)
    key_rot = rotate(key_rot, position).astype(jnp.bfloat16)
    value_rows = (
        jnp.dot(normed, w_value, preferred_element_type=jnp.float32)
        .reshape(row_count, -1, HD)
        .astype(jnp.bfloat16)
    )
    return (query_rot, key_rot, value_rows)


def per_device(tokens, norm_gain, w_query, w_key, w_value, page_counts, pad_counts, page_table):
    row_count = tokens.shape[0]
    stream_total = row_count * lax.axis_size("req")
    longest_prompt = min(8 * row_count, stream_total // 2)
    reach_blocks = min(WINDOW, longest_prompt) // row_count
    block_start = lax.axis_index("req") * row_count
    slot_index = block_start + jnp.arange(row_count, dtype=jnp.int32)
    segment_id, position, is_live = token_meta(slot_index, page_counts, pad_counts)
    query_rot, key_rot, value_rows = project(tokens, norm_gain, w_query, w_key, w_value, position)
    kv_heads = key_rot.shape[1]
    group_size = query_rot.shape[1] // kv_heads
    head_total = kv_heads * group_size
    packed = jnp.concatenate([key_rot, value_rows], axis=-1)

    earlier = [passed_along(packed, "req", shift) for shift in range(reach_blocks, 0, -1)]
    key_blocks = jnp.concatenate(earlier + [packed], axis=0)
    key_count = (reach_blocks + 1) * row_count
    key_index = block_start - reach_blocks * row_count + jnp.arange(key_count, dtype=jnp.int32)
    key_segment, unused_position, key_live = token_meta(key_index, page_counts, pad_counts)
    allowed = (key_segment[None, :] == segment_id[:, None]) & key_live[None, :]
    allowed = (
        allowed
        & (key_index[None, :] <= slot_index[:, None])
        & (slot_index[:, None] - key_index[None, :] < WINDOW)
    )
    score_scale = HD ** (-0.5)
    queries = query_rot.reshape(row_count, kv_heads, group_size, HD)
    keys = key_blocks[..., :HD]
    values = key_blocks[..., HD:]
    scores = (
        jnp.einsum("tgjd,ugd->gjtu", queries, keys, preferred_element_type=jnp.float32)
        * score_scale
    )
    scores = jnp.where(allowed[None, None], scores, MASKED_SCORE)
    row_max = jnp.max(scores, axis=-1, keepdims=True)
    probs = jnp.where(allowed[None, None], jnp.exp(scores - row_max), 0.0)
    prob_total = jnp.sum(probs, axis=-1)
    weights = probs.astype(jnp.bfloat16)
    weighted = jnp.einsum("gjtu,ugd->tgjd", weights, values, preferred_element_type=jnp.float32)
    result = (weighted / jnp.transpose(prob_total, (2, 0, 1))[..., None]).reshape(
        row_count, head_total * HD
    )
    context = jnp.where(is_live[:, None], result, 0.0).astype(jnp.bfloat16)
    live_rows = jnp.where(is_live[:, None, None], packed, jnp.zeros((), jnp.bfloat16))
    page_total = row_count // PAGE
    page_rows = (
        live_rows.reshape(page_total, PAGE, kv_heads, 2 * HD)
        .transpose(0, 2, 1, 3)
        .reshape(page_total, kv_heads, PAGE * 2 * HD)
    )
    tp_count = lax.axis_size("tp")
    slots_here = page_total // tp_count
    local_table = page_table[0]
    slot_hits = (local_table[None, :] == jnp.arange(page_total, dtype=jnp.int32)[:, None]).astype(
        jnp.int32
    )
    page_order = jnp.sum(slot_hits * jnp.arange(page_total, dtype=jnp.int32)[None, :], axis=1)
    page_order = page_order.reshape(tp_count, slots_here).T
    outgoing = page_rows[page_order].reshape(slots_here, tp_count * kv_heads, PAGE * 2 * HD)
    cache = lax.all_to_all(outgoing, "tp", split_axis=1, concat_axis=1, tiled=True)
    return (context, cache)


def solution(mesh):
    in_specs = (
        P("req", None),
        P(),
        P(None, "tp"),
        P(None, "tp"),
        P(None, "tp"),
        P(),
        P(),
        P("req", None),
    )
    out_specs = (P("req", "tp"), P(("req", "tp"), None, None))
    return jax.shard_map(
        per_device, mesh=mesh, in_specs=in_specs, out_specs=out_specs, check_vma=False
    )
```

```python
import functools

import jax
import jax.numpy as jnp
from jax import lax
from jax.experimental import pallas as pl
from jax.experimental.pallas import tpu as pltpu
from jax.sharding import PartitionSpec as P

HD = 80
WINDOW = 4096
PAGE = 16


NORM_EPS = 1e-05
ROPE_BASE = 10000.0
MASKED_SCORE = -1e30


def passed_along(x, axis, by):
    size = lax.axis_size(axis)
    pairs = [(i, i + by) for i in range(size) if 0 <= i + by < size]
    return lax.ppermute(x, axis, pairs)


def token_meta(slot_index, page_counts, pad_counts):
    prompt_count = page_counts.shape[0]
    slot_counts = page_counts * PAGE
    slot_ends = jnp.cumsum(slot_counts)
    segment_id = jnp.sum((slot_index[:, None] >= slot_ends[None, :]).astype(jnp.int32), axis=1)
    one_hot = (segment_id[:, None] == jnp.arange(prompt_count, dtype=jnp.int32)[None, :]).astype(
        jnp.int32
    )
    first_slot = jnp.sum(one_hot * (slot_ends - slot_counts)[None, :], axis=1)
    live_count = jnp.sum(one_hot * (slot_counts - pad_counts)[None, :], axis=1)
    position = slot_index - first_slot
    inside = slot_index >= 0
    is_live = (position < live_count) & inside
    segment_id = jnp.where(inside, segment_id, -1)
    return (segment_id, position, is_live)


def rotate(vectors, position):
    half_width = vectors.shape[-1] // 2
    frequency = ROPE_BASE ** (-2.0 * jnp.arange(half_width, dtype=jnp.float32) / vectors.shape[-1])
    angles = position.astype(jnp.float32)[:, None, None] * frequency[None, None, :]
    cosine = jnp.cos(angles)
    sine_part = jnp.sin(angles)
    front_half = vectors[..., :half_width]
    back_half = vectors[..., half_width:]
    return jnp.concatenate(
        [front_half * cosine - back_half * sine_part, back_half * cosine + front_half * sine_part],
        axis=-1,
    )


def project(tokens, norm_gain, w_query, w_key, w_value, position):
    row_count = tokens.shape[0]
    as_float = tokens.astype(jnp.float32)
    normed = (
        as_float
        * lax.rsqrt(jnp.mean(as_float * as_float, axis=-1, keepdims=True) + NORM_EPS)
        * norm_gain
    ).astype(jnp.bfloat16)
    query_rot = jnp.dot(normed, w_query, preferred_element_type=jnp.float32).reshape(
        row_count, -1, HD
    )
    query_rot = rotate(query_rot, position).astype(jnp.bfloat16)
    key_rot = jnp.dot(normed, w_key, preferred_element_type=jnp.float32).reshape(row_count, -1, HD)
    key_rot = rotate(key_rot, position).astype(jnp.bfloat16)
    value_rows = (
        jnp.dot(normed, w_value, preferred_element_type=jnp.float32)
        .reshape(row_count, -1, HD)
        .astype(jnp.bfloat16)
    )
    return (query_rot, key_rot, value_rows)


def attention_kernel(*refs, block_count, group, rows):
    q_ref, lo_ref, hi_ref, live_ref, kidx_ref = refs[:5]
    kv_refs = refs[5:5 + block_count]
    o_ref = refs[5 + block_count]
    s_scr = refs[6 + block_count]
    scale = HD ** (-0.5)
    queries = q_ref[...]
    low = lo_ref[...]
    high = hi_ref[...]
    row_max = jnp.full((group, rows, 1), MASKED_SCORE, jnp.float32)
    for b in range(block_count):
        keys = kv_refs[b][0]
        key_index = kidx_ref[b:b + 1, :]
        allowed = (key_index >= low) & (key_index <= high)
        tile = lax.dot_general(queries, keys, (((1,), (1,)), ((), ())),
                               preferred_element_type=jnp.float32).reshape(group, rows, -1)
        tile = jnp.where(allowed[None], tile * scale, MASKED_SCORE)
        s_scr[b] = tile
        row_max = jnp.maximum(row_max, jnp.max(tile, axis=-1, keepdims=True))
    total = jnp.zeros((group, rows, 1), jnp.float32)
    weighted = jnp.zeros((group * rows, HD), jnp.float32)
    for b in range(block_count):
        probs = jnp.exp(s_scr[b] - row_max)
        total = total + jnp.sum(probs, axis=-1, keepdims=True)
        weights = probs.astype(jnp.bfloat16).reshape(group * rows, -1)
        weighted = weighted + jnp.dot(weights, kv_refs[b][1], preferred_element_type=jnp.float32)
    result = weighted.reshape(group, rows, HD) / total
    live = live_ref[...] != 0
    o_ref[...] = jnp.where(live[None], result, 0.0).astype(o_ref.dtype).reshape(group * rows, HD)


def attention(queries, low, high, live, key_index, kv_blocks):
    group, rows, _ = queries.shape
    block_count = len(kv_blocks)
    keys_per_block = kv_blocks[0].shape[1]
    kernel = functools.partial(attention_kernel, block_count=block_count, group=group, rows=rows)
    flops = 4 * group * rows * keys_per_block * block_count * HD
    cost = pl.CostEstimate(flops=flops, transcendentals=group * rows * keys_per_block * block_count,
                           bytes_accessed=2 * (queries.size + sum(b.size for b in kv_blocks)) + 2 * queries.size)
    out = pl.pallas_call(
        kernel,
        out_shape=jax.ShapeDtypeStruct((group * rows, HD), jnp.bfloat16),
        scratch_shapes=[pltpu.VMEM((block_count, group, rows, keys_per_block), jnp.float32)],
        compiler_params=pltpu.CompilerParams(vmem_limit_bytes=48 * 1024 * 1024),
        cost_estimate=cost,
    )(queries.reshape(group * rows, HD), low, high, live, key_index, *kv_blocks)
    return out.reshape(group, rows, HD)


def segment_bounds(slot_index, page_counts, pad_counts):
    prompt_count = page_counts.shape[0]
    slot_counts = page_counts * PAGE
    slot_ends = jnp.cumsum(slot_counts)
    segment_id = jnp.sum((slot_index[:, None] >= slot_ends[None, :]).astype(jnp.int32), axis=1)
    one_hot = (segment_id[:, None] == jnp.arange(prompt_count, dtype=jnp.int32)[None, :]).astype(
        jnp.int32
    )
    first_slot = jnp.sum(one_hot * (slot_ends - slot_counts)[None, :], axis=1)
    live_count = jnp.sum(one_hot * (slot_counts - pad_counts)[None, :], axis=1)
    return first_slot, live_count


def per_device(tokens, norm_gain, w_query, w_key, w_value, page_counts, pad_counts, page_table):
    row_count = tokens.shape[0]
    stream_total = row_count * lax.axis_size("req")
    longest_prompt = min(8 * row_count, stream_total // 2)
    reach_blocks = min(WINDOW, longest_prompt) // row_count
    block_start = lax.axis_index("req") * row_count
    slot_index = block_start + jnp.arange(row_count, dtype=jnp.int32)
    segment_id, position, is_live = token_meta(slot_index, page_counts, pad_counts)
    query_rot, key_rot, value_rows = project(tokens, norm_gain, w_query, w_key, w_value, position)
    kv_heads = key_rot.shape[1]
    group_size = query_rot.shape[1] // kv_heads
    head_total = kv_heads * group_size
    packed = jnp.concatenate([key_rot, value_rows], axis=-1)

    first_slot, live_count = segment_bounds(slot_index, page_counts, pad_counts)
    low = jnp.maximum(first_slot, slot_index - WINDOW + 1)[:, None]
    high = jnp.minimum(slot_index, first_slot + live_count - 1)[:, None]
    live_flag = is_live.astype(jnp.int32)[:, None]
    key_count = (reach_blocks + 1) * row_count
    key_index = block_start - reach_blocks * row_count + jnp.arange(key_count, dtype=jnp.int32)
    key_index = key_index.reshape(reach_blocks + 1, row_count)
    per_kv = []
    for kv_id in range(kv_heads):
        own = jnp.stack([key_rot[:, kv_id], value_rows[:, kv_id]], axis=0)
        blocks = [passed_along(own, "req", shift) for shift in range(reach_blocks, 0, -1)]
        head_queries = jnp.transpose(
            query_rot[:, kv_id * group_size:(kv_id + 1) * group_size], (1, 0, 2)
        )
        per_kv.append(attention(head_queries, low, high, live_flag, key_index, blocks + [own]))
    context = jnp.transpose(jnp.concatenate(per_kv, axis=0), (1, 0, 2)).reshape(
        row_count, head_total * HD
    )
    live_rows = jnp.where(is_live[:, None, None], packed, jnp.zeros((), jnp.bfloat16))
    page_total = row_count // PAGE
    page_rows = (
        live_rows.reshape(page_total, PAGE, kv_heads, 2 * HD)
        .transpose(0, 2, 1, 3)
        .reshape(page_total, kv_heads, PAGE * 2 * HD)
    )
    tp_count = lax.axis_size("tp")
    slots_here = page_total // tp_count
    local_table = page_table[0]
    slot_hits = (local_table[None, :] == jnp.arange(page_total, dtype=jnp.int32)[:, None]).astype(
        jnp.int32
    )
    page_order = jnp.sum(slot_hits * jnp.arange(page_total, dtype=jnp.int32)[None, :], axis=1)
    page_order = page_order.reshape(tp_count, slots_here).T
    outgoing = page_rows[page_order].reshape(slots_here, tp_count * kv_heads, PAGE * 2 * HD)
    cache = lax.all_to_all(outgoing, "tp", split_axis=1, concat_axis=1, tiled=True)
    return (context, cache)


def solution(mesh):
    in_specs = (
        P("req", None),
        P(),
        P(None, "tp"),
        P(None, "tp"),
        P(None, "tp"),
        P(),
        P(),
        P("req", None),
    )
    out_specs = (P("req", "tp"), P(("req", "tp"), None, None))
    return jax.shard_map(
        per_device, mesh=mesh, in_specs=in_specs, out_specs=out_specs, check_vma=False
    )
```

```python
import functools

import jax
import jax.numpy as jnp
from jax import lax
from jax.experimental import pallas as pl
from jax.experimental.pallas import tpu as pltpu
from jax.sharding import PartitionSpec as P

HD = 80
WINDOW = 4096
PAGE = 16


NORM_EPS = 1e-05
ROPE_BASE = 10000.0
MASKED_SCORE = -1e30


def passed_along(x, axis, by):
    size = lax.axis_size(axis)
    pairs = [(i, i + by) for i in range(size) if 0 <= i + by < size]
    return lax.ppermute(x, axis, pairs)


def token_meta(slot_index, page_counts, pad_counts):
    prompt_count = page_counts.shape[0]
    slot_counts = page_counts * PAGE
    slot_ends = jnp.cumsum(slot_counts)
    segment_id = jnp.sum((slot_index[:, None] >= slot_ends[None, :]).astype(jnp.int32), axis=1)
    one_hot = (segment_id[:, None] == jnp.arange(prompt_count, dtype=jnp.int32)[None, :]).astype(
        jnp.int32
    )
    first_slot = jnp.sum(one_hot * (slot_ends - slot_counts)[None, :], axis=1)
    live_count = jnp.sum(one_hot * (slot_counts - pad_counts)[None, :], axis=1)
    position = slot_index - first_slot
    inside = slot_index >= 0
    is_live = (position < live_count) & inside
    segment_id = jnp.where(inside, segment_id, -1)
    return (segment_id, position, is_live)


def rotate(vectors, position):
    half_width = vectors.shape[-1] // 2
    frequency = ROPE_BASE ** (-2.0 * jnp.arange(half_width, dtype=jnp.float32) / vectors.shape[-1])
    angles = position.astype(jnp.float32)[:, None, None] * frequency[None, None, :]
    cosine = jnp.cos(angles)
    sine_part = jnp.sin(angles)
    front_half = vectors[..., :half_width]
    back_half = vectors[..., half_width:]
    return jnp.concatenate(
        [front_half * cosine - back_half * sine_part, back_half * cosine + front_half * sine_part],
        axis=-1,
    )


def project(tokens, norm_gain, w_query, w_key, w_value, position):
    row_count = tokens.shape[0]
    as_float = tokens.astype(jnp.float32)
    normed = (
        as_float
        * lax.rsqrt(jnp.mean(as_float * as_float, axis=-1, keepdims=True) + NORM_EPS)
        * norm_gain
    ).astype(jnp.bfloat16)
    query_rot = jnp.dot(normed, w_query, preferred_element_type=jnp.float32).reshape(
        row_count, -1, HD
    )
    query_rot = rotate(query_rot, position).astype(jnp.bfloat16)
    key_rot = jnp.dot(normed, w_key, preferred_element_type=jnp.float32).reshape(row_count, -1, HD)
    key_rot = rotate(key_rot, position).astype(jnp.bfloat16)
    value_rows = (
        jnp.dot(normed, w_value, preferred_element_type=jnp.float32)
        .reshape(row_count, -1, HD)
        .astype(jnp.bfloat16)
    )
    return (query_rot, key_rot, value_rows)


def attention_kernel(*refs, block_count, group, rows):
    q_ref, lo_ref, hi_ref, live_ref, kidx_ref = refs[:5]
    kv_refs = refs[5:5 + block_count]
    o_ref = refs[5 + block_count]
    s_scr = refs[6 + block_count]
    scale = HD ** (-0.5)
    queries = q_ref[...]
    low = lo_ref[...]
    high = hi_ref[...]
    row_max = jnp.full((group, rows, 1), MASKED_SCORE, jnp.float32)
    for b in range(block_count):
        keys = kv_refs[b][:HD, :]
        key_index = kidx_ref[b:b + 1, :]
        allowed = (key_index >= low) & (key_index <= high)
        tile = jnp.dot(queries, keys, preferred_element_type=jnp.float32).reshape(group, rows, -1)
        tile = jnp.where(allowed[None], tile * scale, MASKED_SCORE)
        s_scr[b] = tile
        row_max = jnp.maximum(row_max, jnp.max(tile, axis=-1, keepdims=True))
    total = jnp.zeros((group, rows, 1), jnp.float32)
    weighted = jnp.zeros((group * rows, HD), jnp.float32)
    for b in range(block_count):
        probs = jnp.exp(s_scr[b] - row_max)
        total = total + jnp.sum(probs, axis=-1, keepdims=True)
        weights = probs.astype(jnp.bfloat16).reshape(group * rows, -1)
        weighted = weighted + lax.dot_general(
            weights, kv_refs[b][HD:, :], (((1,), (1,)), ((), ())), preferred_element_type=jnp.float32
        )
    result = weighted.reshape(group, rows, HD) / total
    live = live_ref[...] != 0
    o_ref[...] = jnp.where(live[None], result, 0.0).astype(o_ref.dtype).reshape(group * rows, HD)


def attention(queries, low, high, live, key_index, kv_blocks):
    group, rows, _ = queries.shape
    block_count = len(kv_blocks)
    keys_per_block = kv_blocks[0].shape[1]
    kernel = functools.partial(attention_kernel, block_count=block_count, group=group, rows=rows)
    flops = 4 * group * rows * keys_per_block * block_count * HD
    cost = pl.CostEstimate(flops=flops, transcendentals=group * rows * keys_per_block * block_count,
                           bytes_accessed=2 * (queries.size + sum(b.size for b in kv_blocks)) + 2 * queries.size)
    out = pl.pallas_call(
        kernel,
        out_shape=jax.ShapeDtypeStruct((group * rows, HD), jnp.bfloat16),
        scratch_shapes=[pltpu.VMEM((block_count, group, rows, keys_per_block), jnp.float32)],
        compiler_params=pltpu.CompilerParams(vmem_limit_bytes=48 * 1024 * 1024),
        cost_estimate=cost,
    )(queries.reshape(group * rows, HD), low, high, live, key_index, *kv_blocks)
    return out.reshape(group, rows, HD)


def segment_bounds(slot_index, page_counts, pad_counts):
    prompt_count = page_counts.shape[0]
    slot_counts = page_counts * PAGE
    slot_ends = jnp.cumsum(slot_counts)
    segment_id = jnp.sum((slot_index[:, None] >= slot_ends[None, :]).astype(jnp.int32), axis=1)
    one_hot = (segment_id[:, None] == jnp.arange(prompt_count, dtype=jnp.int32)[None, :]).astype(
        jnp.int32
    )
    first_slot = jnp.sum(one_hot * (slot_ends - slot_counts)[None, :], axis=1)
    live_count = jnp.sum(one_hot * (slot_counts - pad_counts)[None, :], axis=1)
    return first_slot, live_count


def per_device(tokens, norm_gain, w_query, w_key, w_value, page_counts, pad_counts, page_table):
    row_count = tokens.shape[0]
    stream_total = row_count * lax.axis_size("req")
    longest_prompt = min(8 * row_count, stream_total // 2)
    reach_blocks = min(WINDOW, longest_prompt) // row_count
    block_start = lax.axis_index("req") * row_count
    slot_index = block_start + jnp.arange(row_count, dtype=jnp.int32)
    segment_id, position, is_live = token_meta(slot_index, page_counts, pad_counts)
    query_rot, key_rot, value_rows = project(tokens, norm_gain, w_query, w_key, w_value, position)
    kv_heads = key_rot.shape[1]
    group_size = query_rot.shape[1] // kv_heads
    head_total = kv_heads * group_size
    packed = jnp.concatenate([key_rot, value_rows], axis=-1)

    first_slot, live_count = segment_bounds(slot_index, page_counts, pad_counts)
    low = jnp.maximum(first_slot, slot_index - WINDOW + 1)[:, None]
    high = jnp.minimum(slot_index, first_slot + live_count - 1)[:, None]
    live_flag = is_live.astype(jnp.int32)[:, None]
    key_count = (reach_blocks + 1) * row_count
    key_index = block_start - reach_blocks * row_count + jnp.arange(key_count, dtype=jnp.int32)
    key_index = key_index.reshape(reach_blocks + 1, row_count)
    per_kv = []
    for kv_id in range(kv_heads):
        own = jnp.concatenate([key_rot[:, kv_id].T, value_rows[:, kv_id].T], axis=0)
        blocks = [passed_along(own, "req", shift) for shift in range(reach_blocks, 0, -1)]
        head_queries = jnp.transpose(
            query_rot[:, kv_id * group_size:(kv_id + 1) * group_size], (1, 0, 2)
        )
        per_kv.append(attention(head_queries, low, high, live_flag, key_index, blocks + [own]))
    context = jnp.transpose(jnp.concatenate(per_kv, axis=0), (1, 0, 2)).reshape(
        row_count, head_total * HD
    )
    live_rows = jnp.where(is_live[:, None, None], packed, jnp.zeros((), jnp.bfloat16))
    page_total = row_count // PAGE
    page_rows = (
        live_rows.reshape(page_total, PAGE, kv_heads, 2 * HD)
        .transpose(0, 2, 1, 3)
        .reshape(page_total, kv_heads, PAGE * 2 * HD)
    )
    tp_count = lax.axis_size("tp")
    slots_here = page_total // tp_count
    local_table = page_table[0]
    slot_hits = (local_table[None, :] == jnp.arange(page_total, dtype=jnp.int32)[:, None]).astype(
        jnp.int32
    )
    page_order = jnp.sum(slot_hits * jnp.arange(page_total, dtype=jnp.int32)[None, :], axis=1)
    page_order = page_order.reshape(tp_count, slots_here).T
    outgoing = page_rows[page_order].reshape(slots_here, tp_count * kv_heads, PAGE * 2 * HD)
    cache = lax.all_to_all(outgoing, "tp", split_axis=1, concat_axis=1, tiled=True)
    return (context, cache)


def solution(mesh):
    in_specs = (
        P("req", None),
        P(),
        P(None, "tp"),
        P(None, "tp"),
        P(None, "tp"),
        P(),
        P(),
        P("req", None),
    )
    out_specs = (P("req", "tp"), P(("req", "tp"), None, None))
    return jax.shard_map(
        per_device, mesh=mesh, in_specs=in_specs, out_specs=out_specs, check_vma=False
    )
```

```python
import functools

import jax
import jax.numpy as jnp
from jax import lax
from jax.experimental import pallas as pl
from jax.experimental.pallas import tpu as pltpu
from jax.sharding import PartitionSpec as P

HD = 80
WINDOW = 4096
PAGE = 16


NORM_EPS = 1e-05
ROPE_BASE = 10000.0
MASKED_SCORE = -1e30


def passed_along(x, axis, by):
    size = lax.axis_size(axis)
    pairs = [(i, (i + by) % size) for i in range(size)]
    return lax.ppermute(x, axis, pairs)


def token_meta(slot_index, page_counts, pad_counts):
    prompt_count = page_counts.shape[0]
    slot_counts = page_counts * PAGE
    slot_ends = jnp.cumsum(slot_counts)
    segment_id = jnp.sum((slot_index[:, None] >= slot_ends[None, :]).astype(jnp.int32), axis=1)
    one_hot = (segment_id[:, None] == jnp.arange(prompt_count, dtype=jnp.int32)[None, :]).astype(
        jnp.int32
    )
    first_slot = jnp.sum(one_hot * (slot_ends - slot_counts)[None, :], axis=1)
    live_count = jnp.sum(one_hot * (slot_counts - pad_counts)[None, :], axis=1)
    position = slot_index - first_slot
    inside = slot_index >= 0
    is_live = (position < live_count) & inside
    segment_id = jnp.where(inside, segment_id, -1)
    return (segment_id, position, is_live)


def rotate(vectors, position):
    half_width = vectors.shape[-1] // 2
    frequency = ROPE_BASE ** (-2.0 * jnp.arange(half_width, dtype=jnp.float32) / vectors.shape[-1])
    angles = position.astype(jnp.float32)[:, None, None] * frequency[None, None, :]
    cosine = jnp.cos(angles)
    sine_part = jnp.sin(angles)
    front_half = vectors[..., :half_width]
    back_half = vectors[..., half_width:]
    return jnp.concatenate(
        [front_half * cosine - back_half * sine_part, back_half * cosine + front_half * sine_part],
        axis=-1,
    )


def project(tokens, norm_gain, w_query, w_key, w_value, position):
    row_count = tokens.shape[0]
    as_float = tokens.astype(jnp.float32)
    normed = (
        as_float
        * lax.rsqrt(jnp.mean(as_float * as_float, axis=-1, keepdims=True) + NORM_EPS)
        * norm_gain
    ).astype(jnp.bfloat16)
    query_rot = jnp.dot(normed, w_query, preferred_element_type=jnp.float32).reshape(
        row_count, -1, HD
    )
    query_rot = rotate(query_rot, position).astype(jnp.bfloat16)
    key_rot = jnp.dot(normed, w_key, preferred_element_type=jnp.float32).reshape(row_count, -1, HD)
    key_rot = rotate(key_rot, position).astype(jnp.bfloat16)
    value_rows = (
        jnp.dot(normed, w_value, preferred_element_type=jnp.float32)
        .reshape(row_count, -1, HD)
        .astype(jnp.bfloat16)
    )
    return (query_rot, key_rot, value_rows)


def attention_kernel(*refs, block_count, group, rows):
    q_ref, lo_ref, hi_ref, live_ref, kidx_ref = refs[:5]
    kv_refs = refs[5:5 + block_count]
    o_ref = refs[5 + block_count]
    s_scr = refs[6 + block_count]
    scale = HD ** (-0.5)
    queries = q_ref[...]
    low = lo_ref[...]
    high = hi_ref[...]
    row_max = jnp.full((group, rows, 1), MASKED_SCORE, jnp.float32)
    for b in range(block_count):
        keys = kv_refs[b][:HD, :]
        key_index = kidx_ref[b:b + 1, :]
        allowed = (key_index >= low) & (key_index <= high)
        tile = jnp.dot(queries, keys, preferred_element_type=jnp.float32).reshape(group, rows, -1)
        tile = jnp.where(allowed[None], tile * scale, MASKED_SCORE)
        s_scr[b] = tile
        row_max = jnp.maximum(row_max, jnp.max(tile, axis=-1, keepdims=True))
    total = jnp.zeros((group, rows, 1), jnp.float32)
    weighted = jnp.zeros((group * rows, HD), jnp.float32)
    for b in range(block_count):
        probs = jnp.exp(s_scr[b] - row_max)
        total = total + jnp.sum(probs, axis=-1, keepdims=True)
        weights = probs.astype(jnp.bfloat16).reshape(group * rows, -1)
        weighted = weighted + lax.dot_general(
            weights, kv_refs[b][HD:, :], (((1,), (1,)), ((), ())), preferred_element_type=jnp.float32
        )
    result = weighted.reshape(group, rows, HD) / total
    live = live_ref[...] != 0
    o_ref[...] = jnp.where(live[None], result, 0.0).astype(o_ref.dtype).reshape(group * rows, HD)


def attention(queries, low, high, live, key_index, kv_blocks):
    group, rows, _ = queries.shape
    block_count = len(kv_blocks)
    keys_per_block = kv_blocks[0].shape[1]
    kernel = functools.partial(attention_kernel, block_count=block_count, group=group, rows=rows)
    flops = 4 * group * rows * keys_per_block * block_count * HD
    cost = pl.CostEstimate(flops=flops, transcendentals=group * rows * keys_per_block * block_count,
                           bytes_accessed=2 * (queries.size + sum(b.size for b in kv_blocks)) + 2 * queries.size)
    out = pl.pallas_call(
        kernel,
        out_shape=jax.ShapeDtypeStruct((group * rows, HD), jnp.bfloat16),
        scratch_shapes=[pltpu.VMEM((block_count, group, rows, keys_per_block), jnp.float32)],
        compiler_params=pltpu.CompilerParams(vmem_limit_bytes=48 * 1024 * 1024),
        cost_estimate=cost,
    )(queries.reshape(group * rows, HD), low, high, live, key_index, *kv_blocks)
    return out.reshape(group, rows, HD)


def segment_bounds(slot_index, page_counts, pad_counts):
    prompt_count = page_counts.shape[0]
    slot_counts = page_counts * PAGE
    slot_ends = jnp.cumsum(slot_counts)
    segment_id = jnp.sum((slot_index[:, None] >= slot_ends[None, :]).astype(jnp.int32), axis=1)
    one_hot = (segment_id[:, None] == jnp.arange(prompt_count, dtype=jnp.int32)[None, :]).astype(
        jnp.int32
    )
    first_slot = jnp.sum(one_hot * (slot_ends - slot_counts)[None, :], axis=1)
    live_count = jnp.sum(one_hot * (slot_counts - pad_counts)[None, :], axis=1)
    return first_slot, live_count


def per_device(tokens, norm_gain, w_query, w_key, w_value, page_counts, pad_counts, page_table):
    row_count = tokens.shape[0]
    stream_total = row_count * lax.axis_size("req")
    longest_prompt = min(8 * row_count, stream_total // 2)
    reach_blocks = min(WINDOW, longest_prompt) // row_count
    block_start = lax.axis_index("req") * row_count
    slot_index = block_start + jnp.arange(row_count, dtype=jnp.int32)
    segment_id, position, is_live = token_meta(slot_index, page_counts, pad_counts)
    query_rot, key_rot, value_rows = project(tokens, norm_gain, w_query, w_key, w_value, position)
    kv_heads = key_rot.shape[1]
    group_size = query_rot.shape[1] // kv_heads
    head_total = kv_heads * group_size
    packed = jnp.concatenate([key_rot, value_rows], axis=-1)

    first_slot, live_count = segment_bounds(slot_index, page_counts, pad_counts)
    low = jnp.maximum(first_slot, slot_index - WINDOW + 1)[:, None]
    high = jnp.minimum(slot_index, first_slot + live_count - 1)[:, None]
    live_flag = is_live.astype(jnp.int32)[:, None]
    key_count = (reach_blocks + 1) * row_count
    key_index = block_start - reach_blocks * row_count + jnp.arange(key_count, dtype=jnp.int32)
    key_index = key_index.reshape(reach_blocks + 1, row_count)
    per_kv = []
    for kv_id in range(kv_heads):
        own = jnp.concatenate([key_rot[:, kv_id].T, value_rows[:, kv_id].T], axis=0)
        arrived = {shift: passed_along(own, "req", shift) for shift in range(1, reach_blocks + 1)}
        blocks = [arrived[shift] for shift in range(reach_blocks, 0, -1)]
        head_queries = jnp.transpose(
            query_rot[:, kv_id * group_size:(kv_id + 1) * group_size], (1, 0, 2)
        )
        per_kv.append(attention(head_queries, low, high, live_flag, key_index, blocks + [own]))
    context = jnp.transpose(jnp.concatenate(per_kv, axis=0), (1, 0, 2)).reshape(
        row_count, head_total * HD
    )
    live_rows = jnp.where(is_live[:, None, None], packed, jnp.zeros((), jnp.bfloat16))
    page_total = row_count // PAGE
    page_rows = (
        live_rows.reshape(page_total, PAGE, kv_heads, 2 * HD)
        .transpose(0, 2, 1, 3)
        .reshape(page_total, kv_heads, PAGE * 2 * HD)
    )
    tp_count = lax.axis_size("tp")
    slots_here = page_total // tp_count
    every_head = lax.all_gather(page_rows, "tp", axis=1, tiled=True)
    local_table = page_table[0]
    wanted_slot = lax.axis_index("tp") * slots_here + jnp.arange(slots_here, dtype=jnp.int32)
    slot_hits = (local_table[None, :] == wanted_slot[:, None]).astype(jnp.int32)
    page_for_slot = jnp.sum(slot_hits * jnp.arange(page_total, dtype=jnp.int32)[None, :], axis=1)
    cache = every_head[page_for_slot]
    return (context, cache)


def solution(mesh):
    in_specs = (
        P("req", None),
        P(),
        P(None, "tp"),
        P(None, "tp"),
        P(None, "tp"),
        P(),
        P(),
        P("req", None),
    )
    out_specs = (P("req", "tp"), P(("req", "tp"), None, None))
    return jax.shard_map(
        per_device, mesh=mesh, in_specs=in_specs, out_specs=out_specs, check_vma=False
    )
```

```python
import functools

import jax
import jax.numpy as jnp
from jax import lax
from jax.experimental import pallas as pl
from jax.experimental.pallas import tpu as pltpu
from jax.sharding import PartitionSpec as P

HD = 80
WINDOW = 4096
PAGE = 16


NORM_EPS = 1e-05
ROPE_BASE = 10000.0
MASKED_SCORE = -1e30


def passed_along(x, axis, by):
    size = lax.axis_size(axis)
    pairs = [(i, (i + by) % size) for i in range(size)]
    return lax.ppermute(x, axis, pairs)


def token_meta(slot_index, page_counts, pad_counts):
    prompt_count = page_counts.shape[0]
    slot_counts = page_counts * PAGE
    slot_ends = jnp.cumsum(slot_counts)
    segment_id = jnp.sum((slot_index[:, None] >= slot_ends[None, :]).astype(jnp.int32), axis=1)
    one_hot = (segment_id[:, None] == jnp.arange(prompt_count, dtype=jnp.int32)[None, :]).astype(
        jnp.int32
    )
    first_slot = jnp.sum(one_hot * (slot_ends - slot_counts)[None, :], axis=1)
    live_count = jnp.sum(one_hot * (slot_counts - pad_counts)[None, :], axis=1)
    position = slot_index - first_slot
    inside = slot_index >= 0
    is_live = (position < live_count) & inside
    segment_id = jnp.where(inside, segment_id, -1)
    return (segment_id, position, is_live)


def rotate(vectors, position):
    half_width = vectors.shape[-1] // 2
    frequency = ROPE_BASE ** (-2.0 * jnp.arange(half_width, dtype=jnp.float32) / vectors.shape[-1])
    angles = position.astype(jnp.float32)[:, None, None] * frequency[None, None, :]
    cosine = jnp.cos(angles)
    sine_part = jnp.sin(angles)
    front_half = vectors[..., :half_width]
    back_half = vectors[..., half_width:]
    return jnp.concatenate(
        [front_half * cosine - back_half * sine_part, back_half * cosine + front_half * sine_part],
        axis=-1,
    )


def project(tokens, norm_gain, w_query, w_key, w_value, position):
    row_count = tokens.shape[0]
    as_float = tokens.astype(jnp.float32)
    normed = (
        as_float
        * lax.rsqrt(jnp.mean(as_float * as_float, axis=-1, keepdims=True) + NORM_EPS)
        * norm_gain
    ).astype(jnp.bfloat16)
    query_rot = jnp.dot(normed, w_query, preferred_element_type=jnp.float32).reshape(
        row_count, -1, HD
    )
    query_rot = rotate(query_rot, position).astype(jnp.bfloat16)
    key_rot = jnp.dot(normed, w_key, preferred_element_type=jnp.float32).reshape(row_count, -1, HD)
    key_rot = rotate(key_rot, position).astype(jnp.bfloat16)
    value_rows = (
        jnp.dot(normed, w_value, preferred_element_type=jnp.float32)
        .reshape(row_count, -1, HD)
        .astype(jnp.bfloat16)
    )
    return (query_rot, key_rot, value_rows)


def attention_kernel(*refs, block_count, group, rows):
    q_ref, lo_ref, hi_ref, live_ref, kidx_ref = refs[:5]
    kv_refs = refs[5:5 + block_count]
    o_ref = refs[5 + block_count]
    s_scr = refs[6 + block_count]
    scale = HD ** (-0.5)
    queries = q_ref[...]
    low = lo_ref[...]
    high = hi_ref[...]
    row_max = jnp.full((group, rows, 1), MASKED_SCORE, jnp.float32)
    for b in range(block_count):
        keys = kv_refs[b][:HD, :]
        key_index = kidx_ref[b:b + 1, :]
        allowed = (key_index >= low) & (key_index <= high)
        tile = jnp.dot(queries, keys, preferred_element_type=jnp.float32).reshape(group, rows, -1)
        tile = jnp.where(allowed[None], tile * scale, MASKED_SCORE)
        s_scr[b] = tile
        row_max = jnp.maximum(row_max, jnp.max(tile, axis=-1, keepdims=True))
    total = jnp.zeros((group, rows, 1), jnp.float32)
    weighted = jnp.zeros((group * rows, HD), jnp.float32)
    for b in range(block_count):
        probs = jnp.exp(s_scr[b] - row_max)
        total = total + jnp.sum(probs, axis=-1, keepdims=True)
        weights = probs.astype(jnp.bfloat16).reshape(group * rows, -1)
        weighted = weighted + lax.dot_general(
            weights, kv_refs[b][HD:, :], (((1,), (1,)), ((), ())), preferred_element_type=jnp.float32
        )
    result = weighted.reshape(group, rows, HD) / total
    live = live_ref[...] != 0
    o_ref[...] = jnp.where(live[None], result, 0.0).astype(o_ref.dtype).reshape(group * rows, HD)


def attention(queries, low, high, live, key_index, kv_blocks):
    group, rows, _ = queries.shape
    block_count = len(kv_blocks)
    keys_per_block = kv_blocks[0].shape[1]
    kernel = functools.partial(attention_kernel, block_count=block_count, group=group, rows=rows)
    flops = 4 * group * rows * keys_per_block * block_count * HD
    cost = pl.CostEstimate(flops=flops, transcendentals=group * rows * keys_per_block * block_count,
                           bytes_accessed=2 * (queries.size + sum(b.size for b in kv_blocks)) + 2 * queries.size)
    out = pl.pallas_call(
        kernel,
        out_shape=jax.ShapeDtypeStruct((group * rows, HD), jnp.bfloat16),
        scratch_shapes=[pltpu.VMEM((block_count, group, rows, keys_per_block), jnp.float32)],
        compiler_params=pltpu.CompilerParams(vmem_limit_bytes=48 * 1024 * 1024),
        cost_estimate=cost,
    )(queries.reshape(group * rows, HD), low, high, live, key_index, *kv_blocks)
    return out.reshape(group, rows, HD)


def segment_bounds(slot_index, page_counts, pad_counts):
    prompt_count = page_counts.shape[0]
    slot_counts = page_counts * PAGE
    slot_ends = jnp.cumsum(slot_counts)
    segment_id = jnp.sum((slot_index[:, None] >= slot_ends[None, :]).astype(jnp.int32), axis=1)
    one_hot = (segment_id[:, None] == jnp.arange(prompt_count, dtype=jnp.int32)[None, :]).astype(
        jnp.int32
    )
    first_slot = jnp.sum(one_hot * (slot_ends - slot_counts)[None, :], axis=1)
    live_count = jnp.sum(one_hot * (slot_counts - pad_counts)[None, :], axis=1)
    return first_slot, live_count


def per_device(tokens, norm_gain, w_query, w_key, w_value, page_counts, pad_counts, page_table):
    row_count = tokens.shape[0]
    stream_total = row_count * lax.axis_size("req")
    longest_prompt = min(8 * row_count, stream_total // 2)
    reach_blocks = min(WINDOW, longest_prompt) // row_count
    block_start = lax.axis_index("req") * row_count
    slot_index = block_start + jnp.arange(row_count, dtype=jnp.int32)
    segment_id, position, is_live = token_meta(slot_index, page_counts, pad_counts)
    query_rot, key_rot, value_rows = project(tokens, norm_gain, w_query, w_key, w_value, position)
    kv_heads = key_rot.shape[1]
    group_size = query_rot.shape[1] // kv_heads
    head_total = kv_heads * group_size
    packed = jnp.concatenate([key_rot, value_rows], axis=-1)

    first_slot, live_count = segment_bounds(slot_index, page_counts, pad_counts)
    low = jnp.maximum(first_slot, slot_index - WINDOW + 1)[:, None]
    high = jnp.minimum(slot_index, first_slot + live_count - 1)[:, None]
    live_flag = is_live.astype(jnp.int32)[:, None]
    key_count = (reach_blocks + 1) * row_count
    key_index = block_start - reach_blocks * row_count + jnp.arange(key_count, dtype=jnp.int32)
    key_index = key_index.reshape(reach_blocks + 1, row_count)
    per_kv = []
    for kv_id in range(kv_heads):
        own = jnp.concatenate([key_rot[:, kv_id].T, value_rows[:, kv_id].T], axis=0)
        arrived = {shift: passed_along(own, "req", shift) for shift in range(1, reach_blocks + 1)}
        blocks = [arrived[shift] for shift in range(reach_blocks, 0, -1)]
        head_queries = jnp.transpose(
            query_rot[:, kv_id * group_size:(kv_id + 1) * group_size], (1, 0, 2)
        )
        per_kv.append(attention(head_queries, low, high, live_flag, key_index, blocks + [own]))
    context = jnp.transpose(jnp.concatenate(per_kv, axis=0), (1, 0, 2)).reshape(
        row_count, head_total * HD
    )
    live_rows = jnp.where(is_live[:, None, None], packed, jnp.zeros((), jnp.bfloat16))
    page_total = row_count // PAGE
    page_rows = (
        live_rows.reshape(page_total, PAGE, kv_heads, 2 * HD)
        .transpose(0, 2, 1, 3)
        .reshape(page_total, kv_heads, PAGE * 2 * HD)
    )
    tp_count = lax.axis_size("tp")
    slots_here = page_total // tp_count
    local_table = page_table[0]
    slot_hits = (local_table[None, :] == jnp.arange(page_total, dtype=jnp.int32)[:, None]).astype(
        jnp.int32
    )
    page_order = jnp.sum(slot_hits * jnp.arange(page_total, dtype=jnp.int32)[None, :], axis=1)
    page_order = page_order.reshape(tp_count, slots_here).T
    outgoing = page_rows[page_order].reshape(slots_here, tp_count * kv_heads, PAGE * 2 * HD)
    cache = lax.all_to_all(outgoing, "tp", split_axis=1, concat_axis=1, tiled=True)
    return (context, cache)


def solution(mesh):
    in_specs = (
        P("req", None),
        P(),
        P(None, "tp"),
        P(None, "tp"),
        P(None, "tp"),
        P(),
        P(),
        P("req", None),
    )
    out_specs = (P("req", "tp"), P(("req", "tp"), None, None))
    return jax.shard_map(
        per_device, mesh=mesh, in_specs=in_specs, out_specs=out_specs, check_vma=False
    )
```

```python
import functools

import jax
import jax.numpy as jnp
from jax import lax
from jax.experimental import pallas as pl
from jax.experimental.pallas import tpu as pltpu
from jax.sharding import PartitionSpec as P

HD = 80
WINDOW = 4096
PAGE = 16


NORM_EPS = 1e-05
ROPE_BASE = 10000.0
MASKED_SCORE = -1e30


def passed_along(x, axis, by):
    size = lax.axis_size(axis)
    pairs = [(i, (i + by) % size) for i in range(size)]
    return lax.ppermute(x, axis, pairs)


def token_meta(slot_index, page_counts, pad_counts):
    prompt_count = page_counts.shape[0]
    slot_counts = page_counts * PAGE
    slot_ends = jnp.cumsum(slot_counts)
    segment_id = jnp.sum((slot_index[:, None] >= slot_ends[None, :]).astype(jnp.int32), axis=1)
    one_hot = (segment_id[:, None] == jnp.arange(prompt_count, dtype=jnp.int32)[None, :]).astype(
        jnp.int32
    )
    first_slot = jnp.sum(one_hot * (slot_ends - slot_counts)[None, :], axis=1)
    live_count = jnp.sum(one_hot * (slot_counts - pad_counts)[None, :], axis=1)
    position = slot_index - first_slot
    inside = slot_index >= 0
    is_live = (position < live_count) & inside
    segment_id = jnp.where(inside, segment_id, -1)
    return (segment_id, position, is_live)


def rotate(vectors, position):
    half_width = vectors.shape[-1] // 2
    frequency = ROPE_BASE ** (-2.0 * jnp.arange(half_width, dtype=jnp.float32) / vectors.shape[-1])
    angles = position.astype(jnp.float32)[:, None, None] * frequency[None, None, :]
    cosine = jnp.cos(angles)
    sine_part = jnp.sin(angles)
    front_half = vectors[..., :half_width]
    back_half = vectors[..., half_width:]
    return jnp.concatenate(
        [front_half * cosine - back_half * sine_part, back_half * cosine + front_half * sine_part],
        axis=-1,
    )


def project(tokens, norm_gain, w_query, w_key, w_value, position):
    row_count = tokens.shape[0]
    as_float = tokens.astype(jnp.float32)
    normed = (
        as_float
        * lax.rsqrt(jnp.mean(as_float * as_float, axis=-1, keepdims=True) + NORM_EPS)
        * norm_gain
    ).astype(jnp.bfloat16)
    query_rot = jnp.dot(normed, w_query, preferred_element_type=jnp.float32).reshape(
        row_count, -1, HD
    )
    query_rot = rotate(query_rot, position).astype(jnp.bfloat16)
    key_rot = jnp.dot(normed, w_key, preferred_element_type=jnp.float32).reshape(row_count, -1, HD)
    key_rot = rotate(key_rot, position).astype(jnp.bfloat16)
    value_rows = (
        jnp.dot(normed, w_value, preferred_element_type=jnp.float32)
        .reshape(row_count, -1, HD)
        .astype(jnp.bfloat16)
    )
    return (query_rot, key_rot, value_rows)


def attention_kernel(*refs, block_count, group, rows, carry_in, final):
    q_ref, lo_ref, hi_ref, live_ref, kidx_ref = refs[:5]
    at = 5
    if carry_in:
        max_in_ref, total_in_ref, weighted_in_ref = refs[at:at + 3]
        at += 3
    kv_refs = refs[at:at + block_count]
    at += block_count
    out_refs = refs[at:-1]
    s_scr = refs[-1]
    scale = HD ** (-0.5)
    queries = q_ref[...]
    low = lo_ref[...]
    high = hi_ref[...]
    row_max = jnp.full((group, rows, 1), MASKED_SCORE, jnp.float32)
    for b in range(block_count):
        keys = kv_refs[b][:HD, :]
        key_index = kidx_ref[b:b + 1, :]
        allowed = (key_index >= low) & (key_index <= high)
        tile = jnp.dot(queries, keys, preferred_element_type=jnp.float32).reshape(group, rows, -1)
        tile = jnp.where(allowed[None], tile * scale, MASKED_SCORE)
        s_scr[b] = tile
        row_max = jnp.maximum(row_max, jnp.max(tile, axis=-1, keepdims=True))
    if carry_in:
        earlier_max = max_in_ref[...]
        new_max = jnp.maximum(row_max, earlier_max)
        rescale = jnp.exp(earlier_max - new_max)
        total = total_in_ref[...] * rescale
        weighted = weighted_in_ref[...] * rescale.reshape(group * rows, 1)
        row_max = new_max
    else:
        total = jnp.zeros((group, rows, 1), jnp.float32)
        weighted = jnp.zeros((group * rows, HD), jnp.float32)
    for b in range(block_count):
        probs = jnp.exp(s_scr[b] - row_max)
        total = total + jnp.sum(probs, axis=-1, keepdims=True)
        weights = probs.astype(jnp.bfloat16).reshape(group * rows, -1)
        weighted = weighted + lax.dot_general(
            weights, kv_refs[b][HD:, :], (((1,), (1,)), ((), ())), preferred_element_type=jnp.float32
        )
    if final:
        result = weighted.reshape(group, rows, HD) / total
        live = live_ref[...] != 0
        out_refs[0][...] = (
            jnp.where(live[None], result, 0.0).astype(out_refs[0].dtype).reshape(group * rows, HD)
        )
    else:
        out_refs[0][...] = row_max
        out_refs[1][...] = total
        out_refs[2][...] = weighted


def attention_part(queries, low, high, live, key_index, kv_blocks, carry, final):
    group, rows, _ = queries.shape
    block_count = len(kv_blocks)
    keys_per_block = kv_blocks[0].shape[1]
    kernel = functools.partial(
        attention_kernel, block_count=block_count, group=group, rows=rows,
        carry_in=carry is not None, final=final,
    )
    flops = 4 * group * rows * keys_per_block * block_count * HD
    cost = pl.CostEstimate(
        flops=flops,
        transcendentals=group * rows * keys_per_block * block_count,
        bytes_accessed=2 * (queries.size + sum(b.size for b in kv_blocks)) + 2 * queries.size,
    )
    if final:
        out_shape = jax.ShapeDtypeStruct((group * rows, HD), jnp.bfloat16)
    else:
        out_shape = (
            jax.ShapeDtypeStruct((group, rows, 1), jnp.float32),
            jax.ShapeDtypeStruct((group, rows, 1), jnp.float32),
            jax.ShapeDtypeStruct((group * rows, HD), jnp.float32),
        )
    carried = list(carry) if carry is not None else []
    return pl.pallas_call(
        kernel,
        out_shape=out_shape,
        scratch_shapes=[pltpu.VMEM((block_count, group, rows, keys_per_block), jnp.float32)],
        compiler_params=pltpu.CompilerParams(vmem_limit_bytes=48 * 1024 * 1024),
        cost_estimate=cost,
    )(queries.reshape(group * rows, HD), low, high, live, key_index, *carried, *kv_blocks)


def attention(queries, low, high, live, key_index, kv_blocks, late_count):
    group, rows, _ = queries.shape
    early = len(kv_blocks) - late_count
    carry = attention_part(
        queries, low, high, live, key_index[late_count:], kv_blocks[late_count:], None, False
    )
    out = attention_part(
        queries, low, high, live, key_index[:late_count], kv_blocks[:late_count], carry, True
    )
    return out.reshape(group, rows, HD)


def segment_bounds(slot_index, page_counts, pad_counts):
    prompt_count = page_counts.shape[0]
    slot_counts = page_counts * PAGE
    slot_ends = jnp.cumsum(slot_counts)
    segment_id = jnp.sum((slot_index[:, None] >= slot_ends[None, :]).astype(jnp.int32), axis=1)
    one_hot = (segment_id[:, None] == jnp.arange(prompt_count, dtype=jnp.int32)[None, :]).astype(
        jnp.int32
    )
    first_slot = jnp.sum(one_hot * (slot_ends - slot_counts)[None, :], axis=1)
    live_count = jnp.sum(one_hot * (slot_counts - pad_counts)[None, :], axis=1)
    return first_slot, live_count


def per_device(tokens, norm_gain, w_query, w_key, w_value, page_counts, pad_counts, page_table):
    row_count = tokens.shape[0]
    stream_total = row_count * lax.axis_size("req")
    longest_prompt = min(8 * row_count, stream_total // 2)
    reach_blocks = min(WINDOW, longest_prompt) // row_count
    block_start = lax.axis_index("req") * row_count
    slot_index = block_start + jnp.arange(row_count, dtype=jnp.int32)
    segment_id, position, is_live = token_meta(slot_index, page_counts, pad_counts)
    query_rot, key_rot, value_rows = project(tokens, norm_gain, w_query, w_key, w_value, position)
    kv_heads = key_rot.shape[1]
    group_size = query_rot.shape[1] // kv_heads
    head_total = kv_heads * group_size
    packed = jnp.concatenate([key_rot, value_rows], axis=-1)

    first_slot, live_count = segment_bounds(slot_index, page_counts, pad_counts)
    low = jnp.maximum(first_slot, slot_index - WINDOW + 1)[:, None]
    high = jnp.minimum(slot_index, first_slot + live_count - 1)[:, None]
    live_flag = is_live.astype(jnp.int32)[:, None]
    key_count = (reach_blocks + 1) * row_count
    key_index = block_start - reach_blocks * row_count + jnp.arange(key_count, dtype=jnp.int32)
    key_index = key_index.reshape(reach_blocks + 1, row_count)
    per_kv = []
    for kv_id in range(kv_heads):
        own = jnp.concatenate([key_rot[:, kv_id].T, value_rows[:, kv_id].T], axis=0)
        arrived = {shift: passed_along(own, "req", shift) for shift in range(1, reach_blocks + 1)}
        blocks = [arrived[shift] for shift in range(reach_blocks, 0, -1)]
        head_queries = jnp.transpose(
            query_rot[:, kv_id * group_size:(kv_id + 1) * group_size], (1, 0, 2)
        )
        per_kv.append(
            attention(head_queries, low, high, live_flag, key_index, blocks + [own], 2)
        )
    context = jnp.transpose(jnp.concatenate(per_kv, axis=0), (1, 0, 2)).reshape(
        row_count, head_total * HD
    )
    live_rows = jnp.where(is_live[:, None, None], packed, jnp.zeros((), jnp.bfloat16))
    page_total = row_count // PAGE
    page_rows = (
        live_rows.reshape(page_total, PAGE, kv_heads, 2 * HD)
        .transpose(0, 2, 1, 3)
        .reshape(page_total, kv_heads, PAGE * 2 * HD)
    )
    tp_count = lax.axis_size("tp")
    slots_here = page_total // tp_count
    local_table = page_table[0]
    slot_hits = (local_table[None, :] == jnp.arange(page_total, dtype=jnp.int32)[:, None]).astype(
        jnp.int32
    )
    page_order = jnp.sum(slot_hits * jnp.arange(page_total, dtype=jnp.int32)[None, :], axis=1)
    page_order = page_order.reshape(tp_count, slots_here).T
    outgoing = page_rows[page_order].reshape(slots_here, tp_count * kv_heads, PAGE * 2 * HD)
    cache = lax.all_to_all(outgoing, "tp", split_axis=1, concat_axis=1, tiled=True)
    return (context, cache)


def solution(mesh):
    in_specs = (
        P("req", None),
        P(),
        P(None, "tp"),
        P(None, "tp"),
        P(None, "tp"),
        P(),
        P(),
        P("req", None),
    )
    out_specs = (P("req", "tp"), P(("req", "tp"), None, None))
    return jax.shard_map(
        per_device, mesh=mesh, in_specs=in_specs, out_specs=out_specs, check_vma=False
    )
```

```python
import functools

import jax
import jax.numpy as jnp
from jax import lax
from jax.experimental import pallas as pl
from jax.experimental.pallas import tpu as pltpu
from jax.sharding import PartitionSpec as P

HD = 80
WINDOW = 4096
PAGE = 16


NORM_EPS = 1e-05
ROPE_BASE = 10000.0
MASKED_SCORE = -1e30


def passed_along(x, axis, by):
    size = lax.axis_size(axis)
    pairs = [(i, (i + by) % size) for i in range(size)]
    return lax.ppermute(x, axis, pairs)


def running_total(counts):
    order = jnp.arange(counts.shape[0], dtype=jnp.int32)
    upto = order[:, None] >= order[None, :]
    return jnp.sum(jnp.where(upto, counts[None, :], 0), axis=1)


def token_meta(slot_index, page_counts, pad_counts):
    prompt_count = page_counts.shape[0]
    slot_counts = page_counts * PAGE
    slot_ends = running_total(slot_counts)
    segment_id = jnp.sum((slot_index[:, None] >= slot_ends[None, :]).astype(jnp.int32), axis=1)
    one_hot = (segment_id[:, None] == jnp.arange(prompt_count, dtype=jnp.int32)[None, :]).astype(
        jnp.int32
    )
    first_slot = jnp.sum(one_hot * (slot_ends - slot_counts)[None, :], axis=1)
    live_count = jnp.sum(one_hot * (slot_counts - pad_counts)[None, :], axis=1)
    position = slot_index - first_slot
    inside = slot_index >= 0
    is_live = (position < live_count) & inside
    segment_id = jnp.where(inside, segment_id, -1)
    return (segment_id, position, is_live)


def rotate(vectors, position):
    half_width = vectors.shape[-1] // 2
    frequency = ROPE_BASE ** (-2.0 * jnp.arange(half_width, dtype=jnp.float32) / vectors.shape[-1])
    angles = position.astype(jnp.float32)[:, None, None] * frequency[None, None, :]
    cosine = jnp.cos(angles)
    sine_part = jnp.sin(angles)
    front_half = vectors[..., :half_width]
    back_half = vectors[..., half_width:]
    return jnp.concatenate(
        [front_half * cosine - back_half * sine_part, back_half * cosine + front_half * sine_part],
        axis=-1,
    )


def rotate_by_weights(normed, weights, position):
    head_count = weights.shape[1] // HD
    half_width = HD // 2
    split = weights.reshape(weights.shape[0], head_count, 2, half_width)
    swapped = jnp.concatenate([-split[:, :, 1:], split[:, :, :1]], axis=2).reshape(weights.shape)
    direct = jnp.dot(normed, weights, preferred_element_type=jnp.float32)
    partner = jnp.dot(normed, swapped, preferred_element_type=jnp.float32)
    frequency = ROPE_BASE ** (-2.0 * jnp.arange(half_width, dtype=jnp.float32) / HD)
    angles = position.astype(jnp.float32)[:, None] * frequency[None, :]
    cosine = jnp.tile(jnp.cos(angles), (1, 2 * head_count))
    sine_part = jnp.tile(jnp.sin(angles), (1, 2 * head_count))
    rotated = direct * cosine + partner * sine_part
    return rotated.reshape(normed.shape[0], head_count, HD).astype(jnp.bfloat16)


def project(tokens, norm_gain, w_query, w_key, w_value, position):
    row_count = tokens.shape[0]
    as_float = tokens.astype(jnp.float32)
    normed = (
        as_float
        * lax.rsqrt(jnp.mean(as_float * as_float, axis=-1, keepdims=True) + NORM_EPS)
        * norm_gain
    ).astype(jnp.bfloat16)
    query_rot = rotate_by_weights(normed, w_query, position)
    key_rot = jnp.dot(normed, w_key, preferred_element_type=jnp.float32).reshape(row_count, -1, HD)
    key_rot = rotate(key_rot, position).astype(jnp.bfloat16)
    value_rows = (
        jnp.dot(normed, w_value, preferred_element_type=jnp.float32)
        .reshape(row_count, -1, HD)
        .astype(jnp.bfloat16)
    )
    return (query_rot, key_rot, value_rows)


def attention_kernel(*refs, block_count, group, rows, carry_in, final):
    q_ref, lo_ref, hi_ref, live_ref, kidx_ref = refs[:5]
    at = 5
    if carry_in:
        max_in_ref, total_in_ref, weighted_in_ref = refs[at:at + 3]
        at += 3
    kv_refs = refs[at:at + block_count]
    at += block_count
    out_refs = refs[at:-1]
    s_scr = refs[-1]
    scale = HD ** (-0.5)
    queries = q_ref[...]
    low = lo_ref[...]
    high = hi_ref[...]
    row_max = jnp.full((group, rows, 1), MASKED_SCORE, jnp.float32)
    for b in range(block_count):
        keys = kv_refs[b][:HD, :]
        key_index = kidx_ref[b:b + 1, :]
        allowed = (key_index >= low) & (key_index <= high)
        tile = jnp.dot(queries, keys, preferred_element_type=jnp.float32).reshape(group, rows, -1)
        tile = jnp.where(allowed[None], tile * scale, MASKED_SCORE)
        s_scr[b] = tile
        row_max = jnp.maximum(row_max, jnp.max(tile, axis=-1, keepdims=True))
    if carry_in:
        earlier_max = max_in_ref[...]
        new_max = jnp.maximum(row_max, earlier_max)
        rescale = jnp.exp(earlier_max - new_max)
        total = total_in_ref[...] * rescale
        weighted = weighted_in_ref[...] * rescale.reshape(group * rows, 1)
        row_max = new_max
    else:
        total = jnp.zeros((group, rows, 1), jnp.float32)
        weighted = jnp.zeros((group * rows, HD), jnp.float32)
    for b in range(block_count):
        probs = jnp.exp(s_scr[b] - row_max)
        total = total + jnp.sum(probs, axis=-1, keepdims=True)
        weights = probs.astype(jnp.bfloat16).reshape(group * rows, -1)
        weighted = weighted + lax.dot_general(
            weights, kv_refs[b][HD:, :], (((1,), (1,)), ((), ())), preferred_element_type=jnp.float32
        )
    if final:
        result = weighted.reshape(group, rows, HD) / total
        live = live_ref[...] != 0
        out_refs[0][...] = (
            jnp.where(live[None], result, 0.0).astype(out_refs[0].dtype).reshape(group * rows, HD)
        )
    else:
        out_refs[0][...] = row_max
        out_refs[1][...] = total
        out_refs[2][...] = weighted


def attention_part(queries, low, high, live, key_index, kv_blocks, carry, final):
    group, rows, _ = queries.shape
    block_count = len(kv_blocks)
    keys_per_block = kv_blocks[0].shape[1]
    kernel = functools.partial(
        attention_kernel, block_count=block_count, group=group, rows=rows,
        carry_in=carry is not None, final=final,
    )
    flops = 4 * group * rows * keys_per_block * block_count * HD
    cost = pl.CostEstimate(
        flops=flops,
        transcendentals=group * rows * keys_per_block * block_count,
        bytes_accessed=2 * (queries.size + sum(b.size for b in kv_blocks)) + 2 * queries.size,
    )
    if final:
        out_shape = jax.ShapeDtypeStruct((group * rows, HD), jnp.bfloat16)
    else:
        out_shape = (
            jax.ShapeDtypeStruct((group, rows, 1), jnp.float32),
            jax.ShapeDtypeStruct((group, rows, 1), jnp.float32),
            jax.ShapeDtypeStruct((group * rows, HD), jnp.float32),
        )
    carried = list(carry) if carry is not None else []
    return pl.pallas_call(
        kernel,
        out_shape=out_shape,
        scratch_shapes=[pltpu.VMEM((block_count, group, rows, keys_per_block), jnp.float32)],
        compiler_params=pltpu.CompilerParams(vmem_limit_bytes=48 * 1024 * 1024),
        cost_estimate=cost,
    )(queries.reshape(group * rows, HD), low, high, live, key_index, *carried, *kv_blocks)


def attention(queries, low, high, live, key_index, kv_blocks, late_count):
    group, rows, _ = queries.shape
    early = len(kv_blocks) - late_count
    carry = attention_part(
        queries, low, high, live, key_index[late_count:], kv_blocks[late_count:], None, False
    )
    out = attention_part(
        queries, low, high, live, key_index[:late_count], kv_blocks[:late_count], carry, True
    )
    return out.reshape(group, rows, HD)


def segment_bounds(slot_index, page_counts, pad_counts):
    prompt_count = page_counts.shape[0]
    slot_counts = page_counts * PAGE
    slot_ends = running_total(slot_counts)
    segment_id = jnp.sum((slot_index[:, None] >= slot_ends[None, :]).astype(jnp.int32), axis=1)
    one_hot = (segment_id[:, None] == jnp.arange(prompt_count, dtype=jnp.int32)[None, :]).astype(
        jnp.int32
    )
    first_slot = jnp.sum(one_hot * (slot_ends - slot_counts)[None, :], axis=1)
    live_count = jnp.sum(one_hot * (slot_counts - pad_counts)[None, :], axis=1)
    return first_slot, live_count


def per_device(tokens, norm_gain, w_query, w_key, w_value, page_counts, pad_counts, page_table):
    row_count = tokens.shape[0]
    stream_total = row_count * lax.axis_size("req")
    longest_prompt = min(8 * row_count, stream_total // 2)
    reach_blocks = min(WINDOW, longest_prompt) // row_count
    block_start = lax.axis_index("req") * row_count
    slot_index = block_start + jnp.arange(row_count, dtype=jnp.int32)
    segment_id, position, is_live = token_meta(slot_index, page_counts, pad_counts)
    query_rot, key_rot, value_rows = project(tokens, norm_gain, w_query, w_key, w_value, position)
    kv_heads = key_rot.shape[1]
    group_size = query_rot.shape[1] // kv_heads
    head_total = kv_heads * group_size
    packed = jnp.concatenate([key_rot, value_rows], axis=-1)

    first_slot, live_count = segment_bounds(slot_index, page_counts, pad_counts)
    low = jnp.maximum(first_slot, slot_index - WINDOW + 1)[:, None]
    high = jnp.minimum(slot_index, first_slot + live_count - 1)[:, None]
    live_flag = is_live.astype(jnp.int32)[:, None]
    key_count = (reach_blocks + 1) * row_count
    key_index = block_start - reach_blocks * row_count + jnp.arange(key_count, dtype=jnp.int32)
    key_index = key_index.reshape(reach_blocks + 1, row_count)
    per_kv = []
    for kv_id in range(kv_heads):
        own = jnp.concatenate([key_rot[:, kv_id].T, value_rows[:, kv_id].T], axis=0)
        arrived = {shift: passed_along(own, "req", shift) for shift in range(1, reach_blocks + 1)}
        blocks = [arrived[shift] for shift in range(reach_blocks, 0, -1)]
        head_queries = jnp.transpose(
            query_rot[:, kv_id * group_size:(kv_id + 1) * group_size], (1, 0, 2)
        )
        per_kv.append(
            attention(head_queries, low, high, live_flag, key_index, blocks + [own], 2)
        )
    context = jnp.transpose(jnp.concatenate(per_kv, axis=0), (1, 0, 2)).reshape(
        row_count, head_total * HD
    )
    live_rows = jnp.where(is_live[:, None, None], packed, jnp.zeros((), jnp.bfloat16))
    page_total = row_count // PAGE
    page_rows = (
        live_rows.reshape(page_total, PAGE, kv_heads, 2 * HD)
        .transpose(0, 2, 1, 3)
        .reshape(page_total, kv_heads, PAGE * 2 * HD)
    )
    tp_count = lax.axis_size("tp")
    slots_here = page_total // tp_count
    local_table = page_table[0]
    slot_hits = (local_table[None, :] == jnp.arange(page_total, dtype=jnp.int32)[:, None]).astype(
        jnp.int32
    )
    page_order = jnp.sum(slot_hits * jnp.arange(page_total, dtype=jnp.int32)[None, :], axis=1)
    page_order = page_order.reshape(tp_count, slots_here).T
    outgoing = page_rows[page_order].reshape(slots_here, tp_count * kv_heads, PAGE * 2 * HD)
    cache = lax.all_to_all(outgoing, "tp", split_axis=1, concat_axis=1, tiled=True)
    return (context, cache)


def solution(mesh):
    in_specs = (
        P("req", None),
        P(),
        P(None, "tp"),
        P(None, "tp"),
        P(None, "tp"),
        P(),
        P(),
        P("req", None),
    )
    out_specs = (P("req", "tp"), P(("req", "tp"), None, None))
    return jax.shard_map(
        per_device, mesh=mesh, in_specs=in_specs, out_specs=out_specs, check_vma=False
    )
```

```python
import functools

import jax
import jax.numpy as jnp
from jax import lax
from jax.experimental import pallas as pl
from jax.experimental.pallas import tpu as pltpu
from jax.sharding import PartitionSpec as P

HD = 80
WINDOW = 4096
PAGE = 16


NORM_EPS = 1e-05
ROPE_BASE = 10000.0
MASKED_SCORE = -1e30


def passed_along(x, axis, by):
    size = lax.axis_size(axis)
    pairs = [(i, (i + by) % size) for i in range(size)]
    return lax.ppermute(x, axis, pairs)


def running_total(counts):
    order = jnp.arange(counts.shape[0], dtype=jnp.int32)
    upto = order[:, None] >= order[None, :]
    return jnp.sum(jnp.where(upto, counts[None, :], 0), axis=1)


def token_meta(slot_index, page_counts, pad_counts):
    prompt_count = page_counts.shape[0]
    slot_counts = page_counts * PAGE
    slot_ends = running_total(slot_counts)
    segment_id = jnp.sum((slot_index[:, None] >= slot_ends[None, :]).astype(jnp.int32), axis=1)
    one_hot = (segment_id[:, None] == jnp.arange(prompt_count, dtype=jnp.int32)[None, :]).astype(
        jnp.int32
    )
    first_slot = jnp.sum(one_hot * (slot_ends - slot_counts)[None, :], axis=1)
    live_count = jnp.sum(one_hot * (slot_counts - pad_counts)[None, :], axis=1)
    position = slot_index - first_slot
    inside = slot_index >= 0
    is_live = (position < live_count) & inside
    segment_id = jnp.where(inside, segment_id, -1)
    return (segment_id, position, is_live)


def rotate(vectors, position):
    half_width = vectors.shape[-1] // 2
    frequency = ROPE_BASE ** (-2.0 * jnp.arange(half_width, dtype=jnp.float32) / vectors.shape[-1])
    angles = position.astype(jnp.float32)[:, None, None] * frequency[None, None, :]
    cosine = jnp.cos(angles)
    sine_part = jnp.sin(angles)
    front_half = vectors[..., :half_width]
    back_half = vectors[..., half_width:]
    return jnp.concatenate(
        [front_half * cosine - back_half * sine_part, back_half * cosine + front_half * sine_part],
        axis=-1,
    )


def rotate_by_weights(normed, weights, position):
    head_count = weights.shape[1] // HD
    half_width = HD // 2
    split = weights.reshape(weights.shape[0], head_count, 2, half_width)
    swapped = jnp.concatenate([-split[:, :, 1:], split[:, :, :1]], axis=2).reshape(weights.shape)
    direct = jnp.dot(normed, weights, preferred_element_type=jnp.float32)
    partner = jnp.dot(normed, swapped, preferred_element_type=jnp.float32)
    frequency = ROPE_BASE ** (-2.0 * jnp.arange(half_width, dtype=jnp.float32) / HD)
    angles = position.astype(jnp.float32)[:, None] * frequency[None, :]
    cosine = jnp.tile(jnp.cos(angles), (1, 2 * head_count))
    sine_part = jnp.tile(jnp.sin(angles), (1, 2 * head_count))
    rotated = direct * cosine + partner * sine_part
    return rotated.reshape(normed.shape[0], head_count, HD).astype(jnp.bfloat16)


def project(tokens, norm_gain, w_query, w_key, w_value, position):
    row_count = tokens.shape[0]
    as_float = tokens.astype(jnp.float32)
    normed = (
        as_float
        * lax.rsqrt(jnp.mean(as_float * as_float, axis=-1, keepdims=True) + NORM_EPS)
        * norm_gain
    ).astype(jnp.bfloat16)
    query_rot = rotate_by_weights(normed, w_query, position)
    key_rot = jnp.dot(normed, w_key, preferred_element_type=jnp.float32).reshape(row_count, -1, HD)
    key_rot = rotate(key_rot, position).astype(jnp.bfloat16)
    value_rows = (
        jnp.dot(normed, w_value, preferred_element_type=jnp.float32)
        .reshape(row_count, -1, HD)
        .astype(jnp.bfloat16)
    )
    return (query_rot, key_rot, value_rows)


def attention_kernel(*refs, block_count, group, rows, carry_in, final):
    q_ref, lo_ref, hi_ref, live_ref, kidx_ref = refs[:5]
    at = 5
    if carry_in:
        max_in_ref, total_in_ref, weighted_in_ref = refs[at:at + 3]
        at += 3
    kv_refs = refs[at:at + block_count]
    at += block_count
    out_refs = refs[at:-1]
    s_scr = refs[-1]
    scale = HD ** (-0.5)
    queries = q_ref[...]
    low = lo_ref[...]
    high = hi_ref[...]
    row_max = jnp.full((group, rows, 1), MASKED_SCORE, jnp.float32)
    for b in range(block_count):
        keys = kv_refs[b][:HD, :]
        key_index = kidx_ref[b:b + 1, :]
        allowed = (key_index >= low) & (key_index <= high)
        tile = jnp.dot(queries, keys, preferred_element_type=jnp.float32).reshape(group, rows, -1)
        tile = jnp.where(allowed[None], tile * scale, MASKED_SCORE)
        s_scr[b] = tile
        row_max = jnp.maximum(row_max, jnp.max(tile, axis=-1, keepdims=True))
    if carry_in:
        earlier_max = max_in_ref[...]
        new_max = jnp.maximum(row_max, earlier_max)
        rescale = jnp.exp(earlier_max - new_max)
        total = total_in_ref[...] * rescale
        weighted = weighted_in_ref[...] * rescale.reshape(group * rows, 1)
        row_max = new_max
    else:
        total = jnp.zeros((group, rows, 1), jnp.float32)
        weighted = jnp.zeros((group * rows, HD), jnp.float32)
    for b in range(block_count):
        probs = jnp.exp(s_scr[b] - row_max)
        total = total + jnp.sum(probs, axis=-1, keepdims=True)
        weights = probs.astype(jnp.bfloat16).reshape(group * rows, -1)
        weighted = weighted + lax.dot_general(
            weights, kv_refs[b][HD:, :], (((1,), (1,)), ((), ())), preferred_element_type=jnp.float32
        )
    if final:
        result = weighted.reshape(group, rows, HD) / total
        live = live_ref[...] != 0
        result = jnp.where(live[None], result, 0.0).astype(out_refs[0].dtype)
        out_refs[0][...] = jnp.concatenate([result[h] for h in range(group)], axis=1)
    else:
        out_refs[0][...] = row_max
        out_refs[1][...] = total
        out_refs[2][...] = weighted


def attention_part(queries, low, high, live, key_index, kv_blocks, carry, final):
    group, rows, _ = queries.shape
    block_count = len(kv_blocks)
    keys_per_block = kv_blocks[0].shape[1]
    kernel = functools.partial(
        attention_kernel, block_count=block_count, group=group, rows=rows,
        carry_in=carry is not None, final=final,
    )
    flops = 4 * group * rows * keys_per_block * block_count * HD
    cost = pl.CostEstimate(
        flops=flops,
        transcendentals=group * rows * keys_per_block * block_count,
        bytes_accessed=2 * (queries.size + sum(b.size for b in kv_blocks)) + 2 * queries.size,
    )
    if final:
        out_shape = jax.ShapeDtypeStruct((rows, group * HD), jnp.bfloat16)
    else:
        out_shape = (
            jax.ShapeDtypeStruct((group, rows, 1), jnp.float32),
            jax.ShapeDtypeStruct((group, rows, 1), jnp.float32),
            jax.ShapeDtypeStruct((group * rows, HD), jnp.float32),
        )
    carried = list(carry) if carry is not None else []
    return pl.pallas_call(
        kernel,
        out_shape=out_shape,
        scratch_shapes=[pltpu.VMEM((block_count, group, rows, keys_per_block), jnp.float32)],
        compiler_params=pltpu.CompilerParams(vmem_limit_bytes=48 * 1024 * 1024),
        cost_estimate=cost,
    )(queries.reshape(group * rows, HD), low, high, live, key_index, *carried, *kv_blocks)


def attention(queries, low, high, live, key_index, kv_blocks, late_count):
    group, rows, _ = queries.shape
    early = len(kv_blocks) - late_count
    carry = attention_part(
        queries, low, high, live, key_index[late_count:], kv_blocks[late_count:], None, False
    )
    return attention_part(
        queries, low, high, live, key_index[:late_count], kv_blocks[:late_count], carry, True
    )


def segment_bounds(slot_index, page_counts, pad_counts):
    prompt_count = page_counts.shape[0]
    slot_counts = page_counts * PAGE
    slot_ends = running_total(slot_counts)
    segment_id = jnp.sum((slot_index[:, None] >= slot_ends[None, :]).astype(jnp.int32), axis=1)
    one_hot = (segment_id[:, None] == jnp.arange(prompt_count, dtype=jnp.int32)[None, :]).astype(
        jnp.int32
    )
    first_slot = jnp.sum(one_hot * (slot_ends - slot_counts)[None, :], axis=1)
    live_count = jnp.sum(one_hot * (slot_counts - pad_counts)[None, :], axis=1)
    return first_slot, live_count


def per_device(tokens, norm_gain, w_query, w_key, w_value, page_counts, pad_counts, page_table):
    row_count = tokens.shape[0]
    stream_total = row_count * lax.axis_size("req")
    longest_prompt = min(8 * row_count, stream_total // 2)
    reach_blocks = min(WINDOW, longest_prompt) // row_count
    block_start = lax.axis_index("req") * row_count
    slot_index = block_start + jnp.arange(row_count, dtype=jnp.int32)
    segment_id, position, is_live = token_meta(slot_index, page_counts, pad_counts)
    query_rot, key_rot, value_rows = project(tokens, norm_gain, w_query, w_key, w_value, position)
    kv_heads = key_rot.shape[1]
    group_size = query_rot.shape[1] // kv_heads
    head_total = kv_heads * group_size
    packed = jnp.concatenate([key_rot, value_rows], axis=-1)

    first_slot, live_count = segment_bounds(slot_index, page_counts, pad_counts)
    low = jnp.maximum(first_slot, slot_index - WINDOW + 1)[:, None]
    high = jnp.minimum(slot_index, first_slot + live_count - 1)[:, None]
    live_flag = is_live.astype(jnp.int32)[:, None]
    key_count = (reach_blocks + 1) * row_count
    key_index = block_start - reach_blocks * row_count + jnp.arange(key_count, dtype=jnp.int32)
    key_index = key_index.reshape(reach_blocks + 1, row_count)
    live_rows = jnp.where(is_live[:, None, None], packed, jnp.zeros((), jnp.bfloat16))
    page_total = row_count // PAGE
    page_rows = (
        live_rows.reshape(page_total, PAGE, kv_heads, 2 * HD)
        .transpose(0, 2, 1, 3)
        .reshape(page_total, kv_heads, PAGE * 2 * HD)
    )
    tp_count = lax.axis_size("tp")
    slots_here = page_total // tp_count
    local_table = page_table[0]
    slot_hits = (local_table[None, :] == jnp.arange(page_total, dtype=jnp.int32)[:, None]).astype(
        jnp.int32
    )
    page_order = jnp.sum(slot_hits * jnp.arange(page_total, dtype=jnp.int32)[None, :], axis=1)
    page_order = page_order.reshape(tp_count, slots_here).T
    outgoing = page_rows[page_order].reshape(slots_here, tp_count * kv_heads, PAGE * 2 * HD)
    cache = lax.all_to_all(outgoing, "tp", split_axis=1, concat_axis=1, tiled=True)
    owns = [
        jnp.concatenate([key_rot[:, kv_id].T, value_rows[:, kv_id].T], axis=0)
        for kv_id in range(kv_heads)
    ]
    owns, cache = lax.optimization_barrier((owns, cache))
    per_kv = []
    for kv_id in range(kv_heads):
        own = owns[kv_id]
        arrived = {shift: passed_along(own, "req", shift) for shift in range(1, reach_blocks + 1)}
        blocks = [arrived[shift] for shift in range(reach_blocks, 0, -1)]
        head_queries = jnp.transpose(
            query_rot[:, kv_id * group_size:(kv_id + 1) * group_size], (1, 0, 2)
        )
        per_kv.append(
            attention(head_queries, low, high, live_flag, key_index, blocks + [own], 2)
        )
    context = jnp.concatenate(per_kv, axis=1)
    return (context, cache)


def solution(mesh):
    in_specs = (
        P("req", None),
        P(),
        P(None, "tp"),
        P(None, "tp"),
        P(None, "tp"),
        P(),
        P(),
        P("req", None),
    )
    out_specs = (P("req", "tp"), P(("req", "tp"), None, None))
    return jax.shard_map(
        per_device, mesh=mesh, in_specs=in_specs, out_specs=out_specs, check_vma=False
    )
```

```python
import functools

import jax
import jax.numpy as jnp
from jax import lax
from jax.experimental import pallas as pl
from jax.experimental.pallas import tpu as pltpu
from jax.sharding import PartitionSpec as P

HD = 80
WINDOW = 4096
PAGE = 16


NORM_EPS = 1e-05
ROPE_BASE = 10000.0
MASKED_SCORE = -1e30


def passed_along(x, axis, by):
    size = lax.axis_size(axis)
    pairs = [(i, (i + by) % size) for i in range(size)]
    return lax.ppermute(x, axis, pairs)


def running_total(counts):
    order = jnp.arange(counts.shape[0], dtype=jnp.int32)
    upto = order[:, None] >= order[None, :]
    return jnp.sum(jnp.where(upto, counts[None, :], 0), axis=1)


def token_meta(slot_index, page_counts, pad_counts):
    prompt_count = page_counts.shape[0]
    slot_counts = page_counts * PAGE
    slot_ends = running_total(slot_counts)
    segment_id = jnp.sum((slot_index[:, None] >= slot_ends[None, :]).astype(jnp.int32), axis=1)
    one_hot = (segment_id[:, None] == jnp.arange(prompt_count, dtype=jnp.int32)[None, :]).astype(
        jnp.int32
    )
    first_slot = jnp.sum(one_hot * (slot_ends - slot_counts)[None, :], axis=1)
    live_count = jnp.sum(one_hot * (slot_counts - pad_counts)[None, :], axis=1)
    position = slot_index - first_slot
    inside = slot_index >= 0
    is_live = (position < live_count) & inside
    segment_id = jnp.where(inside, segment_id, -1)
    return (segment_id, position, is_live)


def rotate(vectors, position):
    half_width = vectors.shape[-1] // 2
    frequency = ROPE_BASE ** (-2.0 * jnp.arange(half_width, dtype=jnp.float32) / vectors.shape[-1])
    angles = position.astype(jnp.float32)[:, None, None] * frequency[None, None, :]
    cosine = jnp.cos(angles)
    sine_part = jnp.sin(angles)
    front_half = vectors[..., :half_width]
    back_half = vectors[..., half_width:]
    return jnp.concatenate(
        [front_half * cosine - back_half * sine_part, back_half * cosine + front_half * sine_part],
        axis=-1,
    )


def rotate_by_weights(normed, weights, position):
    head_count = weights.shape[1] // HD
    half_width = HD // 2
    split = weights.reshape(weights.shape[0], head_count, 2, half_width)
    swapped = jnp.concatenate([-split[:, :, 1:], split[:, :, :1]], axis=2).reshape(weights.shape)
    direct = jnp.dot(normed, weights, preferred_element_type=jnp.float32)
    partner = jnp.dot(normed, swapped, preferred_element_type=jnp.float32)
    frequency = ROPE_BASE ** (-2.0 * jnp.arange(half_width, dtype=jnp.float32) / HD)
    angles = position.astype(jnp.float32)[:, None] * frequency[None, :]
    cosine = jnp.tile(jnp.cos(angles), (1, 2 * head_count))
    sine_part = jnp.tile(jnp.sin(angles), (1, 2 * head_count))
    rotated = direct * cosine + partner * sine_part
    return rotated.reshape(normed.shape[0], head_count, HD).astype(jnp.bfloat16)


def project(tokens, norm_gain, w_query, w_key, w_value, position):
    row_count = tokens.shape[0]
    as_float = tokens.astype(jnp.float32)
    gram = jnp.dot(tokens, tokens.T, preferred_element_type=jnp.float32)
    on_diagonal = jnp.arange(row_count)[:, None] == jnp.arange(row_count)[None, :]
    square_sum = jnp.sum(jnp.where(on_diagonal, gram, 0.0), axis=-1, keepdims=True)
    normed = (
        as_float * lax.rsqrt(square_sum / tokens.shape[-1] + NORM_EPS) * norm_gain
    ).astype(jnp.bfloat16)
    query_rot = rotate_by_weights(normed, w_query, position)
    key_rot = jnp.dot(normed, w_key, preferred_element_type=jnp.float32).reshape(row_count, -1, HD)
    key_rot = rotate(key_rot, position).astype(jnp.bfloat16)
    value_rows = (
        jnp.dot(normed, w_value, preferred_element_type=jnp.float32)
        .reshape(row_count, -1, HD)
        .astype(jnp.bfloat16)
    )
    return (query_rot, key_rot, value_rows)


def attention_kernel(*refs, block_count, group, rows, carry_in, final):
    q_ref, lo_ref, hi_ref, live_ref, kidx_ref = refs[:5]
    at = 5
    if carry_in:
        max_in_ref, total_in_ref, weighted_in_ref = refs[at:at + 3]
        at += 3
    kv_refs = refs[at:at + block_count]
    at += block_count
    out_refs = refs[at:-1]
    s_scr = refs[-1]
    scale = HD ** (-0.5)
    queries = q_ref[...]
    low = lo_ref[...]
    high = hi_ref[...]
    row_max = jnp.full((group, rows, 1), MASKED_SCORE, jnp.float32)
    for b in range(block_count):
        keys = kv_refs[b][:HD, :]
        key_index = kidx_ref[b:b + 1, :]
        allowed = (key_index >= low) & (key_index <= high)
        tile = jnp.dot(queries, keys, preferred_element_type=jnp.float32).reshape(group, rows, -1)
        tile = jnp.where(allowed[None], tile * scale, MASKED_SCORE)
        s_scr[b] = tile
        row_max = jnp.maximum(row_max, jnp.max(tile, axis=-1, keepdims=True))
    if carry_in:
        earlier_max = max_in_ref[...]
        new_max = jnp.maximum(row_max, earlier_max)
        rescale = jnp.exp(earlier_max - new_max)
        total = total_in_ref[...] * rescale
        weighted = weighted_in_ref[...] * rescale.reshape(group * rows, 1)
        row_max = new_max
    else:
        total = jnp.zeros((group, rows, 1), jnp.float32)
        weighted = jnp.zeros((group * rows, HD), jnp.float32)
    for b in range(block_count):
        probs = jnp.exp(s_scr[b] - row_max)
        total = total + jnp.sum(probs, axis=-1, keepdims=True)
        weights = probs.astype(jnp.bfloat16).reshape(group * rows, -1)
        weighted = weighted + lax.dot_general(
            weights, kv_refs[b][HD:, :], (((1,), (1,)), ((), ())), preferred_element_type=jnp.float32
        )
    if final:
        result = weighted.reshape(group, rows, HD) / total
        live = live_ref[...] != 0
        result = jnp.where(live[None], result, 0.0).astype(out_refs[0].dtype)
        out_refs[0][...] = jnp.concatenate([result[h] for h in range(group)], axis=1)
    else:
        out_refs[0][...] = row_max
        out_refs[1][...] = total
        out_refs[2][...] = weighted


def attention_part(queries, low, high, live, key_index, kv_blocks, carry, final):
    group, rows, _ = queries.shape
    block_count = len(kv_blocks)
    keys_per_block = kv_blocks[0].shape[1]
    kernel = functools.partial(
        attention_kernel, block_count=block_count, group=group, rows=rows,
        carry_in=carry is not None, final=final,
    )
    flops = 4 * group * rows * keys_per_block * block_count * HD
    cost = pl.CostEstimate(
        flops=flops,
        transcendentals=group * rows * keys_per_block * block_count,
        bytes_accessed=2 * (queries.size + sum(b.size for b in kv_blocks)) + 2 * queries.size,
    )
    if final:
        out_shape = jax.ShapeDtypeStruct((rows, group * HD), jnp.bfloat16)
    else:
        out_shape = (
            jax.ShapeDtypeStruct((group, rows, 1), jnp.float32),
            jax.ShapeDtypeStruct((group, rows, 1), jnp.float32),
            jax.ShapeDtypeStruct((group * rows, HD), jnp.float32),
        )
    carried = list(carry) if carry is not None else []
    return pl.pallas_call(
        kernel,
        out_shape=out_shape,
        scratch_shapes=[pltpu.VMEM((block_count, group, rows, keys_per_block), jnp.float32)],
        compiler_params=pltpu.CompilerParams(vmem_limit_bytes=48 * 1024 * 1024),
        cost_estimate=cost,
    )(queries.reshape(group * rows, HD), low, high, live, key_index, *carried, *kv_blocks)


def attention(queries, low, high, live, key_index, kv_blocks, late_count):
    group, rows, _ = queries.shape
    early = len(kv_blocks) - late_count
    carry = attention_part(
        queries, low, high, live, key_index[late_count:], kv_blocks[late_count:], None, False
    )
    return attention_part(
        queries, low, high, live, key_index[:late_count], kv_blocks[:late_count], carry, True
    )


def segment_bounds(slot_index, page_counts, pad_counts):
    prompt_count = page_counts.shape[0]
    slot_counts = page_counts * PAGE
    slot_ends = running_total(slot_counts)
    segment_id = jnp.sum((slot_index[:, None] >= slot_ends[None, :]).astype(jnp.int32), axis=1)
    one_hot = (segment_id[:, None] == jnp.arange(prompt_count, dtype=jnp.int32)[None, :]).astype(
        jnp.int32
    )
    first_slot = jnp.sum(one_hot * (slot_ends - slot_counts)[None, :], axis=1)
    live_count = jnp.sum(one_hot * (slot_counts - pad_counts)[None, :], axis=1)
    return first_slot, live_count


def per_device(tokens, norm_gain, w_query, w_key, w_value, page_counts, pad_counts, page_table):
    row_count = tokens.shape[0]
    stream_total = row_count * lax.axis_size("req")
    longest_prompt = min(8 * row_count, stream_total // 2)
    reach_blocks = min(WINDOW, longest_prompt) // row_count
    block_start = lax.axis_index("req") * row_count
    slot_index = block_start + jnp.arange(row_count, dtype=jnp.int32)
    segment_id, position, is_live = token_meta(slot_index, page_counts, pad_counts)
    query_rot, key_rot, value_rows = project(tokens, norm_gain, w_query, w_key, w_value, position)
    kv_heads = key_rot.shape[1]
    group_size = query_rot.shape[1] // kv_heads
    head_total = kv_heads * group_size
    packed = jnp.concatenate([key_rot, value_rows], axis=-1)

    first_slot, live_count = segment_bounds(slot_index, page_counts, pad_counts)
    low = jnp.maximum(first_slot, slot_index - WINDOW + 1)[:, None]
    high = jnp.minimum(slot_index, first_slot + live_count - 1)[:, None]
    live_flag = is_live.astype(jnp.int32)[:, None]
    key_count = (reach_blocks + 1) * row_count
    key_index = block_start - reach_blocks * row_count + jnp.arange(key_count, dtype=jnp.int32)
    key_index = key_index.reshape(reach_blocks + 1, row_count)
    per_kv = []
    for kv_id in range(kv_heads):
        own = jnp.concatenate([key_rot[:, kv_id].T, value_rows[:, kv_id].T], axis=0)
        arrived = {shift: passed_along(own, "req", shift) for shift in range(1, reach_blocks + 1)}
        blocks = [arrived[shift] for shift in range(reach_blocks, 0, -1)]
        head_queries = jnp.transpose(
            query_rot[:, kv_id * group_size:(kv_id + 1) * group_size], (1, 0, 2)
        )
        per_kv.append(
            attention(head_queries, low, high, live_flag, key_index, blocks + [own], 2)
        )
    context = jnp.concatenate(per_kv, axis=1)
    live_rows = jnp.where(is_live[:, None, None], packed, jnp.zeros((), jnp.bfloat16))
    page_total = row_count // PAGE
    page_rows = (
        live_rows.reshape(page_total, PAGE, kv_heads, 2 * HD)
        .transpose(0, 2, 1, 3)
        .reshape(page_total, kv_heads, PAGE * 2 * HD)
    )
    tp_count = lax.axis_size("tp")
    slots_here = page_total // tp_count
    local_table = page_table[0]
    slot_hits = (local_table[None, :] == jnp.arange(page_total, dtype=jnp.int32)[:, None]).astype(
        jnp.int32
    )
    page_order = jnp.sum(slot_hits * jnp.arange(page_total, dtype=jnp.int32)[None, :], axis=1)
    page_order = page_order.reshape(tp_count, slots_here).T
    outgoing = page_rows[page_order].reshape(slots_here, tp_count * kv_heads, PAGE * 2 * HD)
    cache = lax.all_to_all(outgoing, "tp", split_axis=1, concat_axis=1, tiled=True)
    return (context, cache)


def solution(mesh):
    in_specs = (
        P("req", None),
        P(),
        P(None, "tp"),
        P(None, "tp"),
        P(None, "tp"),
        P(),
        P(),
        P("req", None),
    )
    out_specs = (P("req", "tp"), P(("req", "tp"), None, None))
    return jax.shard_map(
        per_device, mesh=mesh, in_specs=in_specs, out_specs=out_specs, check_vma=False
    )
```

```python
import functools

import jax
import jax.numpy as jnp
from jax import lax
from jax.experimental import pallas as pl
from jax.experimental.pallas import tpu as pltpu
from jax.sharding import PartitionSpec as P

HD = 80
WINDOW = 4096
PAGE = 16


NORM_EPS = 1e-05
ROPE_BASE = 10000.0
MASKED_SCORE = -1e30


def passed_along(x, axis, by):
    size = lax.axis_size(axis)
    pairs = [(i, (i + by) % size) for i in range(size)]
    return lax.ppermute(x, axis, pairs)


def running_total(counts):
    order = jnp.arange(counts.shape[0], dtype=jnp.int32)
    upto = order[:, None] >= order[None, :]
    return jnp.sum(jnp.where(upto, counts[None, :], 0), axis=1)


def token_meta(slot_index, page_counts, pad_counts):
    prompt_count = page_counts.shape[0]
    slot_counts = page_counts * PAGE
    slot_ends = running_total(slot_counts)
    segment_id = jnp.sum((slot_index[:, None] >= slot_ends[None, :]).astype(jnp.int32), axis=1)
    one_hot = (segment_id[:, None] == jnp.arange(prompt_count, dtype=jnp.int32)[None, :]).astype(
        jnp.int32
    )
    first_slot = jnp.sum(one_hot * (slot_ends - slot_counts)[None, :], axis=1)
    live_count = jnp.sum(one_hot * (slot_counts - pad_counts)[None, :], axis=1)
    position = slot_index - first_slot
    inside = slot_index >= 0
    is_live = (position < live_count) & inside
    segment_id = jnp.where(inside, segment_id, -1)
    return (segment_id, position, is_live)


def rotate(vectors, position):
    half_width = vectors.shape[-1] // 2
    frequency = ROPE_BASE ** (-2.0 * jnp.arange(half_width, dtype=jnp.float32) / vectors.shape[-1])
    angles = position.astype(jnp.float32)[:, None, None] * frequency[None, None, :]
    cosine = jnp.cos(angles)
    sine_part = jnp.sin(angles)
    front_half = vectors[..., :half_width]
    back_half = vectors[..., half_width:]
    return jnp.concatenate(
        [front_half * cosine - back_half * sine_part, back_half * cosine + front_half * sine_part],
        axis=-1,
    )


def rotate_by_weights(normed, weights, position):
    head_count = weights.shape[1] // HD
    half_width = HD // 2
    split = weights.reshape(weights.shape[0], head_count, 2, half_width)
    swapped = jnp.concatenate([-split[:, :, 1:], split[:, :, :1]], axis=2).reshape(weights.shape)
    direct = jnp.dot(normed, weights, preferred_element_type=jnp.float32)
    partner = jnp.dot(normed, swapped, preferred_element_type=jnp.float32)
    frequency = ROPE_BASE ** (-2.0 * jnp.arange(half_width, dtype=jnp.float32) / HD)
    angles = position.astype(jnp.float32)[:, None] * frequency[None, :]
    cosine = jnp.tile(jnp.cos(angles), (1, 2 * head_count))
    sine_part = jnp.tile(jnp.sin(angles), (1, 2 * head_count))
    rotated = direct * cosine + partner * sine_part
    return rotated.reshape(normed.shape[0], head_count, HD).astype(jnp.bfloat16)


def project(tokens, norm_gain, w_query, w_key, w_value, position):
    row_count = tokens.shape[0]
    as_float = tokens.astype(jnp.float32)
    gram = jnp.dot(tokens, tokens.T, preferred_element_type=jnp.float32)
    on_diagonal = jnp.arange(row_count)[:, None] == jnp.arange(row_count)[None, :]
    square_sum = jnp.sum(jnp.where(on_diagonal, gram, 0.0), axis=-1, keepdims=True)
    normed = (
        as_float * lax.rsqrt(square_sum / tokens.shape[-1] + NORM_EPS) * norm_gain
    ).astype(jnp.bfloat16)
    query_rot = rotate_by_weights(normed, w_query, position)
    key_rot = jnp.dot(normed, w_key, preferred_element_type=jnp.float32).reshape(row_count, -1, HD)
    key_rot = rotate(key_rot, position).astype(jnp.bfloat16)
    value_rows = (
        jnp.dot(normed, w_value, preferred_element_type=jnp.float32)
        .reshape(row_count, -1, HD)
        .astype(jnp.bfloat16)
    )
    return (query_rot, key_rot, value_rows)


def attention_kernel(*refs, block_count, group, rows, carry_in, final):
    q_ref, lo_ref, hi_ref, live_ref, kidx_ref, need_ref = refs[:6]
    at = 6
    if carry_in:
        max_in_ref, total_in_ref, weighted_in_ref = refs[at:at + 3]
        at += 3
    kv_refs = refs[at:at + block_count]
    at += block_count
    out_refs = refs[at:-1]
    s_scr = refs[-1]
    scale = HD ** (-0.5)
    queries = q_ref[...]
    low = lo_ref[...]
    high = hi_ref[...]
    row_max = jnp.full((group, rows, 1), MASKED_SCORE, jnp.float32)
    for b in range(block_count):

        def score_block(running_max, b=b):
            keys = kv_refs[b][:HD, :]
            key_index = kidx_ref[b:b + 1, :]
            allowed = (key_index >= low) & (key_index <= high)
            tile = jnp.dot(queries, keys, preferred_element_type=jnp.float32)
            tile = jnp.where(allowed[None], tile.reshape(group, rows, -1) * scale, MASKED_SCORE)
            s_scr[b] = tile
            return jnp.maximum(running_max, jnp.max(tile, axis=-1, keepdims=True))

        row_max = lax.cond(need_ref[b] != 0, score_block, lambda m: m, row_max)
    if carry_in:
        earlier_max = max_in_ref[...]
        new_max = jnp.maximum(row_max, earlier_max)
        rescale = jnp.exp(earlier_max - new_max)
        total = total_in_ref[...] * rescale
        weighted = weighted_in_ref[...] * rescale.reshape(group * rows, 1)
        row_max = new_max
    else:
        total = jnp.zeros((group, rows, 1), jnp.float32)
        weighted = jnp.zeros((group * rows, HD), jnp.float32)
    for b in range(block_count):

        def take_block(state, b=b):
            block_total, block_weighted = state
            probs = jnp.exp(s_scr[b] - row_max)
            block_total = block_total + jnp.sum(probs, axis=-1, keepdims=True)
            weights = probs.astype(jnp.bfloat16).reshape(group * rows, -1)
            block_weighted = block_weighted + lax.dot_general(
                weights, kv_refs[b][HD:, :], (((1,), (1,)), ((), ())),
                preferred_element_type=jnp.float32,
            )
            return block_total, block_weighted

        total, weighted = lax.cond(need_ref[b] != 0, take_block, lambda st: st, (total, weighted))
    if final:
        result = weighted.reshape(group, rows, HD) / total
        live = live_ref[...] != 0
        result = jnp.where(live[None], result, 0.0).astype(out_refs[0].dtype)
        out_refs[0][...] = jnp.concatenate([result[h] for h in range(group)], axis=1)
    else:
        out_refs[0][...] = row_max
        out_refs[1][...] = total
        out_refs[2][...] = weighted


def attention_part(queries, low, high, live, key_index, kv_blocks, carry, final):
    group, rows, _ = queries.shape
    block_count = len(kv_blocks)
    keys_per_block = kv_blocks[0].shape[1]
    kernel = functools.partial(
        attention_kernel, block_count=block_count, group=group, rows=rows,
        carry_in=carry is not None, final=final,
    )
    flops = 4 * group * rows * keys_per_block * block_count * HD
    cost = pl.CostEstimate(
        flops=flops,
        transcendentals=group * rows * keys_per_block * block_count,
        bytes_accessed=2 * (queries.size + sum(b.size for b in kv_blocks)) + 2 * queries.size,
    )
    if final:
        out_shape = jax.ShapeDtypeStruct((rows, group * HD), jnp.bfloat16)
    else:
        out_shape = (
            jax.ShapeDtypeStruct((group, rows, 1), jnp.float32),
            jax.ShapeDtypeStruct((group, rows, 1), jnp.float32),
            jax.ShapeDtypeStruct((group * rows, HD), jnp.float32),
        )
    carried = list(carry) if carry is not None else []
    valid = low <= high
    need = jnp.any(
        valid
        & (low <= key_index[:, -1][None, :])
        & (high >= key_index[:, 0][None, :]),
        axis=0,
    ).astype(jnp.int32)
    vmem = pl.BlockSpec(memory_space=pltpu.VMEM)
    in_specs = [vmem] * 5 + [pl.BlockSpec(memory_space=pltpu.SMEM)]
    in_specs += [vmem] * (len(carried) + block_count)
    return pl.pallas_call(
        kernel,
        out_shape=out_shape,
        in_specs=in_specs,
        scratch_shapes=[pltpu.VMEM((block_count, group, rows, keys_per_block), jnp.float32)],
        compiler_params=pltpu.CompilerParams(vmem_limit_bytes=48 * 1024 * 1024),
        cost_estimate=cost,
    )(queries.reshape(group * rows, HD), low, high, live, key_index, need, *carried, *kv_blocks)


def attention(queries, low, high, live, key_index, kv_blocks, late_count):
    group, rows, _ = queries.shape
    early = len(kv_blocks) - late_count
    carry = attention_part(
        queries, low, high, live, key_index[late_count:], kv_blocks[late_count:], None, False
    )
    return attention_part(
        queries, low, high, live, key_index[:late_count], kv_blocks[:late_count], carry, True
    )


def segment_bounds(slot_index, page_counts, pad_counts):
    prompt_count = page_counts.shape[0]
    slot_counts = page_counts * PAGE
    slot_ends = running_total(slot_counts)
    segment_id = jnp.sum((slot_index[:, None] >= slot_ends[None, :]).astype(jnp.int32), axis=1)
    one_hot = (segment_id[:, None] == jnp.arange(prompt_count, dtype=jnp.int32)[None, :]).astype(
        jnp.int32
    )
    first_slot = jnp.sum(one_hot * (slot_ends - slot_counts)[None, :], axis=1)
    live_count = jnp.sum(one_hot * (slot_counts - pad_counts)[None, :], axis=1)
    return first_slot, live_count


def per_device(tokens, norm_gain, w_query, w_key, w_value, page_counts, pad_counts, page_table):
    row_count = tokens.shape[0]
    stream_total = row_count * lax.axis_size("req")
    longest_prompt = min(8 * row_count, stream_total // 2)
    reach_blocks = min(WINDOW, longest_prompt) // row_count
    block_start = lax.axis_index("req") * row_count
    slot_index = block_start + jnp.arange(row_count, dtype=jnp.int32)
    segment_id, position, is_live = token_meta(slot_index, page_counts, pad_counts)
    query_rot, key_rot, value_rows = project(tokens, norm_gain, w_query, w_key, w_value, position)
    kv_heads = key_rot.shape[1]
    group_size = query_rot.shape[1] // kv_heads
    head_total = kv_heads * group_size
    packed = jnp.concatenate([key_rot, value_rows], axis=-1)

    first_slot, live_count = segment_bounds(slot_index, page_counts, pad_counts)
    low = jnp.maximum(first_slot, slot_index - WINDOW + 1)[:, None]
    high = jnp.minimum(slot_index, first_slot + live_count - 1)[:, None]
    live_flag = is_live.astype(jnp.int32)[:, None]
    key_count = (reach_blocks + 1) * row_count
    key_index = block_start - reach_blocks * row_count + jnp.arange(key_count, dtype=jnp.int32)
    key_index = key_index.reshape(reach_blocks + 1, row_count)
    per_kv = []
    for kv_id in range(kv_heads):
        own = jnp.concatenate([key_rot[:, kv_id].T, value_rows[:, kv_id].T], axis=0)
        arrived = {shift: passed_along(own, "req", shift) for shift in range(1, reach_blocks + 1)}
        blocks = [arrived[shift] for shift in range(reach_blocks, 0, -1)]
        head_queries = jnp.transpose(
            query_rot[:, kv_id * group_size:(kv_id + 1) * group_size], (1, 0, 2)
        )
        per_kv.append(
            attention(head_queries, low, high, live_flag, key_index, blocks + [own], 2)
        )
    context = jnp.concatenate(per_kv, axis=1)
    live_rows = jnp.where(is_live[:, None, None], packed, jnp.zeros((), jnp.bfloat16))
    page_total = row_count // PAGE
    page_rows = (
        live_rows.reshape(page_total, PAGE, kv_heads, 2 * HD)
        .transpose(0, 2, 1, 3)
        .reshape(page_total, kv_heads, PAGE * 2 * HD)
    )
    tp_count = lax.axis_size("tp")
    slots_here = page_total // tp_count
    local_table = page_table[0]
    slot_hits = (local_table[None, :] == jnp.arange(page_total, dtype=jnp.int32)[:, None]).astype(
        jnp.int32
    )
    page_order = jnp.sum(slot_hits * jnp.arange(page_total, dtype=jnp.int32)[None, :], axis=1)
    page_order = page_order.reshape(tp_count, slots_here).T
    outgoing = page_rows[page_order].reshape(slots_here, tp_count * kv_heads, PAGE * 2 * HD)
    cache = lax.all_to_all(outgoing, "tp", split_axis=1, concat_axis=1, tiled=True)
    return (context, cache)


def solution(mesh):
    in_specs = (
        P("req", None),
        P(),
        P(None, "tp"),
        P(None, "tp"),
        P(None, "tp"),
        P(),
        P(),
        P("req", None),
    )
    out_specs = (P("req", "tp"), P(("req", "tp"), None, None))
    return jax.shard_map(
        per_device, mesh=mesh, in_specs=in_specs, out_specs=out_specs, check_vma=False
    )
```

```python
import functools

import jax
import jax.numpy as jnp
from jax import lax
from jax.experimental import pallas as pl
from jax.experimental.pallas import tpu as pltpu
from jax.sharding import PartitionSpec as P

HD = 80
WINDOW = 4096
PAGE = 16


NORM_EPS = 1e-05
ROPE_BASE = 10000.0
MASKED_SCORE = -1e30


def passed_along(x, axis, by):
    size = lax.axis_size(axis)
    pairs = [(i, (i + by) % size) for i in range(size)]
    return lax.ppermute(x, axis, pairs)


def issue_order(reach_blocks):
    leading = [shift for shift in (4, 8) if shift <= reach_blocks]
    return leading + [shift for shift in range(1, reach_blocks + 1) if shift not in leading]


def running_total(counts):
    order = jnp.arange(counts.shape[0], dtype=jnp.int32)
    upto = order[:, None] >= order[None, :]
    return jnp.sum(jnp.where(upto, counts[None, :], 0), axis=1)


def token_meta(slot_index, page_counts, pad_counts):
    prompt_count = page_counts.shape[0]
    slot_counts = page_counts * PAGE
    slot_ends = running_total(slot_counts)
    segment_id = jnp.sum((slot_index[:, None] >= slot_ends[None, :]).astype(jnp.int32), axis=1)
    one_hot = (segment_id[:, None] == jnp.arange(prompt_count, dtype=jnp.int32)[None, :]).astype(
        jnp.int32
    )
    first_slot = jnp.sum(one_hot * (slot_ends - slot_counts)[None, :], axis=1)
    live_count = jnp.sum(one_hot * (slot_counts - pad_counts)[None, :], axis=1)
    position = slot_index - first_slot
    inside = slot_index >= 0
    is_live = (position < live_count) & inside
    segment_id = jnp.where(inside, segment_id, -1)
    return (segment_id, position, is_live)


def rotate(vectors, position):
    half_width = vectors.shape[-1] // 2
    frequency = ROPE_BASE ** (-2.0 * jnp.arange(half_width, dtype=jnp.float32) / vectors.shape[-1])
    angles = position.astype(jnp.float32)[:, None, None] * frequency[None, None, :]
    cosine = jnp.cos(angles)
    sine_part = jnp.sin(angles)
    front_half = vectors[..., :half_width]
    back_half = vectors[..., half_width:]
    return jnp.concatenate(
        [front_half * cosine - back_half * sine_part, back_half * cosine + front_half * sine_part],
        axis=-1,
    )


def rotate_by_weights(normed, weights, position):
    head_count = weights.shape[1] // HD
    half_width = HD // 2
    split = weights.reshape(weights.shape[0], head_count, 2, half_width)
    swapped = jnp.concatenate([-split[:, :, 1:], split[:, :, :1]], axis=2).reshape(weights.shape)
    direct = jnp.dot(normed, weights, preferred_element_type=jnp.float32)
    partner = jnp.dot(normed, swapped, preferred_element_type=jnp.float32)
    frequency = ROPE_BASE ** (-2.0 * jnp.arange(half_width, dtype=jnp.float32) / HD)
    angles = position.astype(jnp.float32)[:, None] * frequency[None, :]
    cosine = jnp.tile(jnp.cos(angles), (1, 2 * head_count))
    sine_part = jnp.tile(jnp.sin(angles), (1, 2 * head_count))
    rotated = direct * cosine + partner * sine_part
    return rotated.reshape(normed.shape[0], head_count, HD).astype(jnp.bfloat16)


def project(tokens, norm_gain, w_query, w_key, w_value, position):
    row_count = tokens.shape[0]
    as_float = tokens.astype(jnp.float32)
    gram = jnp.dot(tokens, tokens.T, preferred_element_type=jnp.float32)
    on_diagonal = jnp.arange(row_count)[:, None] == jnp.arange(row_count)[None, :]
    square_sum = jnp.sum(jnp.where(on_diagonal, gram, 0.0), axis=-1, keepdims=True)
    normed = (
        as_float * lax.rsqrt(square_sum / tokens.shape[-1] + NORM_EPS) * norm_gain
    ).astype(jnp.bfloat16)
    query_rot = rotate_by_weights(normed, w_query, position)
    key_rot = jnp.dot(normed, w_key, preferred_element_type=jnp.float32).reshape(row_count, -1, HD)
    key_rot = rotate(key_rot, position).astype(jnp.bfloat16)
    value_rows = (
        jnp.dot(normed, w_value, preferred_element_type=jnp.float32)
        .reshape(row_count, -1, HD)
        .astype(jnp.bfloat16)
    )
    return (query_rot, key_rot, value_rows)


def attention_kernel(*refs, block_count, group, rows, carry_in, final):
    q_ref, lo_ref, hi_ref, live_ref, kidx_ref = refs[:5]
    at = 5
    if carry_in:
        max_in_ref, total_in_ref, weighted_in_ref = refs[at:at + 3]
        at += 3
    kv_refs = refs[at:at + block_count]
    at += block_count
    out_refs = refs[at:-1]
    s_scr = refs[-1]
    scale = HD ** (-0.5)
    queries = q_ref[...]
    low = lo_ref[...]
    high = hi_ref[...]
    row_max = jnp.full((group, rows, 1), MASKED_SCORE, jnp.float32)
    for b in range(block_count):
        keys = kv_refs[b][:HD, :]
        key_index = kidx_ref[b:b + 1, :]
        allowed = (key_index >= low) & (key_index <= high)
        tile = jnp.dot(queries, keys, preferred_element_type=jnp.float32).reshape(group, rows, -1)
        tile = jnp.where(allowed[None], tile * scale, MASKED_SCORE)
        s_scr[b] = tile
        row_max = jnp.maximum(row_max, jnp.max(tile, axis=-1, keepdims=True))
    if carry_in:
        earlier_max = max_in_ref[...]
        new_max = jnp.maximum(row_max, earlier_max)
        rescale = jnp.exp(earlier_max - new_max)
        total = total_in_ref[...] * rescale
        weighted = weighted_in_ref[...] * rescale.reshape(group * rows, 1)
        row_max = new_max
    else:
        total = jnp.zeros((group, rows, 1), jnp.float32)
        weighted = jnp.zeros((group * rows, HD), jnp.float32)
    for b in range(block_count):
        probs = jnp.exp(s_scr[b] - row_max)
        total = total + jnp.sum(probs, axis=-1, keepdims=True)
        weights = probs.astype(jnp.bfloat16).reshape(group * rows, -1)
        weighted = weighted + lax.dot_general(
            weights, kv_refs[b][HD:, :], (((1,), (1,)), ((), ())), preferred_element_type=jnp.float32
        )
    if final:
        result = weighted.reshape(group, rows, HD) / total
        live = live_ref[...] != 0
        result = jnp.where(live[None], result, 0.0).astype(out_refs[0].dtype)
        out_refs[0][...] = jnp.concatenate([result[h] for h in range(group)], axis=1)
    else:
        out_refs[0][...] = row_max
        out_refs[1][...] = total
        out_refs[2][...] = weighted


def attention_part(queries, low, high, live, key_index, kv_blocks, carry, final):
    group, rows, _ = queries.shape
    block_count = len(kv_blocks)
    keys_per_block = kv_blocks[0].shape[1]
    kernel = functools.partial(
        attention_kernel, block_count=block_count, group=group, rows=rows,
        carry_in=carry is not None, final=final,
    )
    flops = 4 * group * rows * keys_per_block * block_count * HD
    cost = pl.CostEstimate(
        flops=flops,
        transcendentals=group * rows * keys_per_block * block_count,
        bytes_accessed=2 * (queries.size + sum(b.size for b in kv_blocks)) + 2 * queries.size,
    )
    if final:
        out_shape = jax.ShapeDtypeStruct((rows, group * HD), jnp.bfloat16)
    else:
        out_shape = (
            jax.ShapeDtypeStruct((group, rows, 1), jnp.float32),
            jax.ShapeDtypeStruct((group, rows, 1), jnp.float32),
            jax.ShapeDtypeStruct((group * rows, HD), jnp.float32),
        )
    carried = list(carry) if carry is not None else []
    return pl.pallas_call(
        kernel,
        out_shape=out_shape,
        scratch_shapes=[pltpu.VMEM((block_count, group, rows, keys_per_block), jnp.float32)],
        compiler_params=pltpu.CompilerParams(vmem_limit_bytes=48 * 1024 * 1024),
        cost_estimate=cost,
    )(queries.reshape(group * rows, HD), low, high, live, key_index, *carried, *kv_blocks)


def attention(queries, low, high, live, key_index, kv_blocks, late_count):
    group, rows, _ = queries.shape
    early = len(kv_blocks) - late_count
    carry = attention_part(
        queries, low, high, live, key_index[late_count:], kv_blocks[late_count:], None, False
    )
    return attention_part(
        queries, low, high, live, key_index[:late_count], kv_blocks[:late_count], carry, True
    )


def segment_bounds(slot_index, page_counts, pad_counts):
    prompt_count = page_counts.shape[0]
    slot_counts = page_counts * PAGE
    slot_ends = running_total(slot_counts)
    segment_id = jnp.sum((slot_index[:, None] >= slot_ends[None, :]).astype(jnp.int32), axis=1)
    one_hot = (segment_id[:, None] == jnp.arange(prompt_count, dtype=jnp.int32)[None, :]).astype(
        jnp.int32
    )
    first_slot = jnp.sum(one_hot * (slot_ends - slot_counts)[None, :], axis=1)
    live_count = jnp.sum(one_hot * (slot_counts - pad_counts)[None, :], axis=1)
    return first_slot, live_count


def per_device(tokens, norm_gain, w_query, w_key, w_value, page_counts, pad_counts, page_table):
    row_count = tokens.shape[0]
    stream_total = row_count * lax.axis_size("req")
    longest_prompt = min(8 * row_count, stream_total // 2)
    reach_blocks = min(WINDOW, longest_prompt) // row_count
    block_start = lax.axis_index("req") * row_count
    slot_index = block_start + jnp.arange(row_count, dtype=jnp.int32)
    segment_id, position, is_live = token_meta(slot_index, page_counts, pad_counts)
    query_rot, key_rot, value_rows = project(tokens, norm_gain, w_query, w_key, w_value, position)
    kv_heads = key_rot.shape[1]
    group_size = query_rot.shape[1] // kv_heads
    head_total = kv_heads * group_size
    packed = jnp.concatenate([key_rot, value_rows], axis=-1)

    first_slot, live_count = segment_bounds(slot_index, page_counts, pad_counts)
    low = jnp.maximum(first_slot, slot_index - WINDOW + 1)[:, None]
    high = jnp.minimum(slot_index, first_slot + live_count - 1)[:, None]
    live_flag = is_live.astype(jnp.int32)[:, None]
    key_count = (reach_blocks + 1) * row_count
    key_index = block_start - reach_blocks * row_count + jnp.arange(key_count, dtype=jnp.int32)
    key_index = key_index.reshape(reach_blocks + 1, row_count)
    per_kv = []
    for kv_id in range(kv_heads):
        own = jnp.concatenate([key_rot[:, kv_id].T, value_rows[:, kv_id].T], axis=0)
        arrived = {shift: passed_along(own, "req", shift) for shift in issue_order(reach_blocks)}
        blocks = [arrived[shift] for shift in range(reach_blocks, 0, -1)]
        head_queries = jnp.transpose(
            query_rot[:, kv_id * group_size:(kv_id + 1) * group_size], (1, 0, 2)
        )
        per_kv.append(
            attention(head_queries, low, high, live_flag, key_index, blocks + [own], 2)
        )
    context = jnp.concatenate(per_kv, axis=1)
    live_rows = jnp.where(is_live[:, None, None], packed, jnp.zeros((), jnp.bfloat16))
    page_total = row_count // PAGE
    page_rows = (
        live_rows.reshape(page_total, PAGE, kv_heads, 2 * HD)
        .transpose(0, 2, 1, 3)
        .reshape(page_total, kv_heads, PAGE * 2 * HD)
    )
    tp_count = lax.axis_size("tp")
    slots_here = page_total // tp_count
    local_table = page_table[0]
    slot_hits = (local_table[None, :] == jnp.arange(page_total, dtype=jnp.int32)[:, None]).astype(
        jnp.int32
    )
    page_order = jnp.sum(slot_hits * jnp.arange(page_total, dtype=jnp.int32)[None, :], axis=1)
    page_order = page_order.reshape(tp_count, slots_here).T
    outgoing = page_rows[page_order].reshape(slots_here, tp_count * kv_heads, PAGE * 2 * HD)
    cache = lax.all_to_all(outgoing, "tp", split_axis=1, concat_axis=1, tiled=True)
    return (context, cache)


def solution(mesh):
    in_specs = (
        P("req", None),
        P(),
        P(None, "tp"),
        P(None, "tp"),
        P(None, "tp"),
        P(),
        P(),
        P("req", None),
    )
    out_specs = (P("req", "tp"), P(("req", "tp"), None, None))
    return jax.shard_map(
        per_device, mesh=mesh, in_specs=in_specs, out_specs=out_specs, check_vma=False
    )
```

```python
import functools

import jax
import jax.numpy as jnp
from jax import lax
from jax.experimental import pallas as pl
from jax.experimental.pallas import tpu as pltpu
from jax.sharding import PartitionSpec as P

HD = 80
WINDOW = 4096
PAGE = 16


NORM_EPS = 1e-05
ROPE_BASE = 10000.0
MASKED_SCORE = -1e30


def passed_along(x, axis, by):
    size = lax.axis_size(axis)
    pairs = [(i, (i + by) % size) for i in range(size)]
    return lax.ppermute(x, axis, pairs)


def issue_order(reach_blocks):
    leading = [shift for shift in (4, 8) if shift <= reach_blocks]
    return leading + [shift for shift in range(1, reach_blocks + 1) if shift not in leading]


def running_total(counts):
    order = jnp.arange(counts.shape[0], dtype=jnp.int32)
    upto = order[:, None] >= order[None, :]
    return jnp.sum(jnp.where(upto, counts[None, :], 0), axis=1)


def token_meta(slot_index, page_counts, pad_counts):
    prompt_count = page_counts.shape[0]
    slot_counts = page_counts * PAGE
    slot_ends = running_total(slot_counts)
    segment_id = jnp.sum((slot_index[:, None] >= slot_ends[None, :]).astype(jnp.int32), axis=1)
    one_hot = (segment_id[:, None] == jnp.arange(prompt_count, dtype=jnp.int32)[None, :]).astype(
        jnp.int32
    )
    first_slot = jnp.sum(one_hot * (slot_ends - slot_counts)[None, :], axis=1)
    live_count = jnp.sum(one_hot * (slot_counts - pad_counts)[None, :], axis=1)
    position = slot_index - first_slot
    inside = slot_index >= 0
    is_live = (position < live_count) & inside
    segment_id = jnp.where(inside, segment_id, -1)
    return (segment_id, position, is_live)


def rotate(vectors, position):
    half_width = vectors.shape[-1] // 2
    frequency = ROPE_BASE ** (-2.0 * jnp.arange(half_width, dtype=jnp.float32) / vectors.shape[-1])
    angles = position.astype(jnp.float32)[:, None, None] * frequency[None, None, :]
    cosine = jnp.cos(angles)
    sine_part = jnp.sin(angles)
    front_half = vectors[..., :half_width]
    back_half = vectors[..., half_width:]
    return jnp.concatenate(
        [front_half * cosine - back_half * sine_part, back_half * cosine + front_half * sine_part],
        axis=-1,
    )


def rotate_by_weights(normed, weights, position):
    head_count = weights.shape[1] // HD
    half_width = HD // 2
    split = weights.reshape(weights.shape[0], head_count, 2, half_width)
    swapped = jnp.concatenate([-split[:, :, 1:], split[:, :, :1]], axis=2).reshape(weights.shape)
    direct = jnp.dot(normed, weights, preferred_element_type=jnp.float32)
    partner = jnp.dot(normed, swapped, preferred_element_type=jnp.float32)
    frequency = ROPE_BASE ** (-2.0 * jnp.arange(half_width, dtype=jnp.float32) / HD)
    angles = position.astype(jnp.float32)[:, None] * frequency[None, :]
    cosine = jnp.tile(jnp.cos(angles), (1, 2 * head_count))
    sine_part = jnp.tile(jnp.sin(angles), (1, 2 * head_count))
    rotated = direct * cosine + partner * sine_part
    return rotated.reshape(normed.shape[0], head_count, HD).astype(jnp.bfloat16)


def project(tokens, norm_gain, w_query, w_key, w_value, position):
    row_count = tokens.shape[0]
    as_float = tokens.astype(jnp.float32)
    normed = (
        as_float
        * lax.rsqrt(jnp.mean(as_float * as_float, axis=-1, keepdims=True) + NORM_EPS)
        * norm_gain
    ).astype(jnp.bfloat16)
    query_rot = rotate_by_weights(normed, w_query, position)
    key_rot = jnp.dot(normed, w_key, preferred_element_type=jnp.float32).reshape(row_count, -1, HD)
    key_rot = rotate(key_rot, position).astype(jnp.bfloat16)
    value_rows = (
        jnp.dot(normed, w_value, preferred_element_type=jnp.float32)
        .reshape(row_count, -1, HD)
        .astype(jnp.bfloat16)
    )
    return (query_rot, key_rot, value_rows)


def attention_kernel(*refs, block_count, group, rows, carry_in, final):
    q_ref, lo_ref, hi_ref, live_ref, kidx_ref = refs[:5]
    at = 5
    if carry_in:
        max_in_ref, total_in_ref, weighted_in_ref = refs[at:at + 3]
        at += 3
    kv_refs = refs[at:at + block_count]
    at += block_count
    out_refs = refs[at:-1]
    s_scr = refs[-1]
    scale = HD ** (-0.5)
    queries = q_ref[...]
    low = lo_ref[...]
    high = hi_ref[...]
    row_max = jnp.full((group, rows, 1), MASKED_SCORE, jnp.float32)
    for b in range(block_count):
        keys = kv_refs[b][:HD, :]
        key_index = kidx_ref[b:b + 1, :]
        allowed = (key_index >= low) & (key_index <= high)
        tile = jnp.dot(queries, keys, preferred_element_type=jnp.float32).reshape(group, rows, -1)
        tile = jnp.where(allowed[None], tile * scale, MASKED_SCORE)
        s_scr[b] = tile
        row_max = jnp.maximum(row_max, jnp.max(tile, axis=-1, keepdims=True))
    if carry_in:
        earlier_max = max_in_ref[...]
        new_max = jnp.maximum(row_max, earlier_max)
        rescale = jnp.exp(earlier_max - new_max)
        total = total_in_ref[...] * rescale
        weighted = weighted_in_ref[...] * rescale.reshape(group * rows, 1)
        row_max = new_max
    else:
        total = jnp.zeros((group, rows, 1), jnp.float32)
        weighted = jnp.zeros((group * rows, HD), jnp.float32)
    for b in range(block_count):
        probs = jnp.exp(s_scr[b] - row_max)
        total = total + jnp.sum(probs, axis=-1, keepdims=True)
        weights = probs.astype(jnp.bfloat16).reshape(group * rows, -1)
        weighted = weighted + lax.dot_general(
            weights, kv_refs[b][HD:, :], (((1,), (1,)), ((), ())), preferred_element_type=jnp.float32
        )
    if final:
        result = weighted.reshape(group, rows, HD) / total
        live = live_ref[...] != 0
        out_refs[0][...] = (
            jnp.where(live[None], result, 0.0).astype(out_refs[0].dtype).reshape(group * rows, HD)
        )
    else:
        out_refs[0][...] = row_max
        out_refs[1][...] = total
        out_refs[2][...] = weighted


def attention_part(queries, low, high, live, key_index, kv_blocks, carry, final):
    group, rows, _ = queries.shape
    block_count = len(kv_blocks)
    keys_per_block = kv_blocks[0].shape[1]
    kernel = functools.partial(
        attention_kernel, block_count=block_count, group=group, rows=rows,
        carry_in=carry is not None, final=final,
    )
    flops = 4 * group * rows * keys_per_block * block_count * HD
    cost = pl.CostEstimate(
        flops=flops,
        transcendentals=group * rows * keys_per_block * block_count,
        bytes_accessed=2 * (queries.size + sum(b.size for b in kv_blocks)) + 2 * queries.size,
    )
    if final:
        out_shape = jax.ShapeDtypeStruct((group * rows, HD), jnp.bfloat16)
    else:
        out_shape = (
            jax.ShapeDtypeStruct((group, rows, 1), jnp.float32),
            jax.ShapeDtypeStruct((group, rows, 1), jnp.float32),
            jax.ShapeDtypeStruct((group * rows, HD), jnp.float32),
        )
    carried = list(carry) if carry is not None else []
    return pl.pallas_call(
        kernel,
        out_shape=out_shape,
        scratch_shapes=[pltpu.VMEM((block_count, group, rows, keys_per_block), jnp.float32)],
        compiler_params=pltpu.CompilerParams(vmem_limit_bytes=48 * 1024 * 1024),
        cost_estimate=cost,
    )(queries.reshape(group * rows, HD), low, high, live, key_index, *carried, *kv_blocks)


def attention(queries, low, high, live, key_index, kv_blocks, late_count):
    group, rows, _ = queries.shape
    early = len(kv_blocks) - late_count
    carry = attention_part(
        queries, low, high, live, key_index[late_count:], kv_blocks[late_count:], None, False
    )
    out = attention_part(
        queries, low, high, live, key_index[:late_count], kv_blocks[:late_count], carry, True
    )
    return out.reshape(group, rows, HD)


def segment_bounds(slot_index, page_counts, pad_counts):
    prompt_count = page_counts.shape[0]
    slot_counts = page_counts * PAGE
    slot_ends = running_total(slot_counts)
    segment_id = jnp.sum((slot_index[:, None] >= slot_ends[None, :]).astype(jnp.int32), axis=1)
    one_hot = (segment_id[:, None] == jnp.arange(prompt_count, dtype=jnp.int32)[None, :]).astype(
        jnp.int32
    )
    first_slot = jnp.sum(one_hot * (slot_ends - slot_counts)[None, :], axis=1)
    live_count = jnp.sum(one_hot * (slot_counts - pad_counts)[None, :], axis=1)
    return first_slot, live_count


def per_device(tokens, norm_gain, w_query, w_key, w_value, page_counts, pad_counts, page_table):
    row_count = tokens.shape[0]
    stream_total = row_count * lax.axis_size("req")
    longest_prompt = min(8 * row_count, stream_total // 2)
    reach_blocks = min(WINDOW, longest_prompt) // row_count
    block_start = lax.axis_index("req") * row_count
    slot_index = block_start + jnp.arange(row_count, dtype=jnp.int32)
    segment_id, position, is_live = token_meta(slot_index, page_counts, pad_counts)
    query_rot, key_rot, value_rows = project(tokens, norm_gain, w_query, w_key, w_value, position)
    kv_heads = key_rot.shape[1]
    group_size = query_rot.shape[1] // kv_heads
    head_total = kv_heads * group_size
    packed = jnp.concatenate([key_rot, value_rows], axis=-1)

    first_slot, live_count = segment_bounds(slot_index, page_counts, pad_counts)
    low = jnp.maximum(first_slot, slot_index - WINDOW + 1)[:, None]
    high = jnp.minimum(slot_index, first_slot + live_count - 1)[:, None]
    live_flag = is_live.astype(jnp.int32)[:, None]
    key_count = (reach_blocks + 1) * row_count
    key_index = block_start - reach_blocks * row_count + jnp.arange(key_count, dtype=jnp.int32)
    key_index = key_index.reshape(reach_blocks + 1, row_count)
    per_kv = []
    for kv_id in range(kv_heads):
        own = jnp.concatenate([key_rot[:, kv_id].T, value_rows[:, kv_id].T], axis=0)
        arrived = {shift: passed_along(own, "req", shift) for shift in issue_order(reach_blocks)}
        blocks = [arrived[shift] for shift in range(reach_blocks, 0, -1)]
        head_queries = jnp.transpose(
            query_rot[:, kv_id * group_size:(kv_id + 1) * group_size], (1, 0, 2)
        )
        per_kv.append(
            attention(head_queries, low, high, live_flag, key_index, blocks + [own], 2)
        )
    context = jnp.transpose(jnp.concatenate(per_kv, axis=0), (1, 0, 2)).reshape(
        row_count, head_total * HD
    )
    live_rows = jnp.where(is_live[:, None, None], packed, jnp.zeros((), jnp.bfloat16))
    page_total = row_count // PAGE
    page_rows = (
        live_rows.reshape(page_total, PAGE, kv_heads, 2 * HD)
        .transpose(0, 2, 1, 3)
        .reshape(page_total, kv_heads, PAGE * 2 * HD)
    )
    tp_count = lax.axis_size("tp")
    slots_here = page_total // tp_count
    local_table = page_table[0]
    slot_hits = (local_table[None, :] == jnp.arange(page_total, dtype=jnp.int32)[:, None]).astype(
        jnp.int32
    )
    page_order = jnp.sum(slot_hits * jnp.arange(page_total, dtype=jnp.int32)[None, :], axis=1)
    page_order = page_order.reshape(tp_count, slots_here).T
    outgoing = page_rows[page_order].reshape(slots_here, tp_count * kv_heads, PAGE * 2 * HD)
    cache = lax.all_to_all(outgoing, "tp", split_axis=1, concat_axis=1, tiled=True)
    return (context, cache)


def solution(mesh):
    in_specs = (
        P("req", None),
        P(),
        P(None, "tp"),
        P(None, "tp"),
        P(None, "tp"),
        P(),
        P(),
        P("req", None),
    )
    out_specs = (P("req", "tp"), P(("req", "tp"), None, None))
    return jax.shard_map(
        per_device, mesh=mesh, in_specs=in_specs, out_specs=out_specs, check_vma=False
    )
```

```python
import functools

import jax
import jax.numpy as jnp
from jax import lax
from jax.experimental import pallas as pl
from jax.experimental.pallas import tpu as pltpu
from jax.sharding import PartitionSpec as P

HD = 80
WINDOW = 4096
PAGE = 16


NORM_EPS = 1e-05
ROPE_BASE = 10000.0
MASKED_SCORE = -1e30


def passed_along(x, axis, by):
    size = lax.axis_size(axis)
    pairs = [(i, (i + by) % size) for i in range(size)]
    return lax.ppermute(x, axis, pairs)


def running_total(counts):
    order = jnp.arange(counts.shape[0], dtype=jnp.int32)
    upto = order[:, None] >= order[None, :]
    return jnp.sum(jnp.where(upto, counts[None, :], 0), axis=1)


def token_meta(slot_index, page_counts, pad_counts):
    prompt_count = page_counts.shape[0]
    slot_counts = page_counts * PAGE
    slot_ends = running_total(slot_counts)
    segment_id = jnp.sum((slot_index[:, None] >= slot_ends[None, :]).astype(jnp.int32), axis=1)
    one_hot = (segment_id[:, None] == jnp.arange(prompt_count, dtype=jnp.int32)[None, :]).astype(
        jnp.int32
    )
    first_slot = jnp.sum(one_hot * (slot_ends - slot_counts)[None, :], axis=1)
    live_count = jnp.sum(one_hot * (slot_counts - pad_counts)[None, :], axis=1)
    position = slot_index - first_slot
    inside = slot_index >= 0
    is_live = (position < live_count) & inside
    segment_id = jnp.where(inside, segment_id, -1)
    return (segment_id, position, is_live)


def rotate(vectors, position):
    half_width = vectors.shape[-1] // 2
    frequency = ROPE_BASE ** (-2.0 * jnp.arange(half_width, dtype=jnp.float32) / vectors.shape[-1])
    angles = position.astype(jnp.float32)[:, None, None] * frequency[None, None, :]
    cosine = jnp.cos(angles)
    sine_part = jnp.sin(angles)
    front_half = vectors[..., :half_width]
    back_half = vectors[..., half_width:]
    return jnp.concatenate(
        [front_half * cosine - back_half * sine_part, back_half * cosine + front_half * sine_part],
        axis=-1,
    )


def rotate_by_weights(normed, weights, position):
    head_count = weights.shape[1] // HD
    half_width = HD // 2
    split = weights.reshape(weights.shape[0], head_count, 2, half_width)
    swapped = jnp.concatenate([-split[:, :, 1:], split[:, :, :1]], axis=2).reshape(weights.shape)
    direct = jnp.dot(normed, weights, preferred_element_type=jnp.float32)
    partner = jnp.dot(normed, swapped, preferred_element_type=jnp.float32)
    frequency = ROPE_BASE ** (-2.0 * jnp.arange(half_width, dtype=jnp.float32) / HD)
    angles = position.astype(jnp.float32)[:, None] * frequency[None, :]
    cosine = jnp.tile(jnp.cos(angles), (1, 2 * head_count))
    sine_part = jnp.tile(jnp.sin(angles), (1, 2 * head_count))
    rotated = direct * cosine + partner * sine_part
    return rotated.reshape(normed.shape[0], head_count, HD).astype(jnp.bfloat16)


def project(tokens, norm_gain, w_query, w_key, w_value, position):
    row_count = tokens.shape[0]
    as_float = tokens.astype(jnp.float32)
    normed = (
        as_float
        * lax.rsqrt(jnp.mean(as_float * as_float, axis=-1, keepdims=True) + NORM_EPS)
        * norm_gain
    ).astype(jnp.bfloat16)
    query_rot = rotate_by_weights(normed, w_query, position)
    key_rot = jnp.dot(normed, w_key, preferred_element_type=jnp.float32).reshape(row_count, -1, HD)
    key_rot = rotate(key_rot, position).astype(jnp.bfloat16)
    value_rows = (
        jnp.dot(normed, w_value, preferred_element_type=jnp.float32)
        .reshape(row_count, -1, HD)
        .astype(jnp.bfloat16)
    )
    return (query_rot, key_rot, value_rows)


def attention_kernel(*refs, block_count, group, rows, carry_in, final):
    q_ref, lo_ref, hi_ref, live_ref, kidx_ref = refs[:5]
    at = 5
    if carry_in:
        max_in_ref, total_in_ref, weighted_in_ref = refs[at:at + 3]
        at += 3
    kv_refs = refs[at:at + block_count]
    at += block_count
    out_refs = refs[at:-1]
    s_scr = refs[-1]
    scale = HD ** (-0.5)
    queries = q_ref[...]
    low = lo_ref[...]
    high = hi_ref[...]
    row_max = jnp.full((group, rows, 1), MASKED_SCORE, jnp.float32)
    for b in range(block_count):
        keys = kv_refs[b][:HD, :]
        key_index = kidx_ref[b:b + 1, :]
        allowed = (key_index >= low) & (key_index <= high)
        tile = jnp.dot(queries, keys, preferred_element_type=jnp.float32).reshape(group, rows, -1)
        tile = jnp.where(allowed[None], tile * scale, MASKED_SCORE)
        s_scr[b] = tile
        row_max = jnp.maximum(row_max, jnp.max(tile, axis=-1, keepdims=True))
    if carry_in:
        earlier_max = max_in_ref[...]
        new_max = jnp.maximum(row_max, earlier_max)
        rescale = jnp.exp(earlier_max - new_max)
        total = total_in_ref[...] * rescale
        weighted = weighted_in_ref[...] * rescale.reshape(group * rows, 1)
        row_max = new_max
    else:
        total = jnp.zeros((group, rows, 1), jnp.float32)
        weighted = jnp.zeros((group * rows, HD), jnp.float32)
    for b in range(block_count):
        probs = jnp.exp(s_scr[b] - row_max)
        total = total + jnp.sum(probs, axis=-1, keepdims=True)
        weights = probs.astype(jnp.bfloat16).reshape(group * rows, -1)
        weighted = weighted + lax.dot_general(
            weights, kv_refs[b][HD:, :], (((1,), (1,)), ((), ())), preferred_element_type=jnp.float32
        )
    if final:
        result = weighted.reshape(group, rows, HD) / total
        live = live_ref[...] != 0
        out_refs[0][...] = (
            jnp.where(live[None], result, 0.0).astype(out_refs[0].dtype).reshape(group * rows, HD)
        )
    else:
        out_refs[0][...] = row_max
        out_refs[1][...] = total
        out_refs[2][...] = weighted


def attention_part(queries, low, high, live, key_index, kv_blocks, carry, final):
    group, rows, _ = queries.shape
    block_count = len(kv_blocks)
    keys_per_block = kv_blocks[0].shape[1]
    kernel = functools.partial(
        attention_kernel, block_count=block_count, group=group, rows=rows,
        carry_in=carry is not None, final=final,
    )
    flops = 4 * group * rows * keys_per_block * block_count * HD
    cost = pl.CostEstimate(
        flops=flops,
        transcendentals=group * rows * keys_per_block * block_count,
        bytes_accessed=2 * (queries.size + sum(b.size for b in kv_blocks)) + 2 * queries.size,
    )
    if final:
        out_shape = jax.ShapeDtypeStruct((group * rows, HD), jnp.bfloat16)
    else:
        out_shape = (
            jax.ShapeDtypeStruct((group, rows, 1), jnp.float32),
            jax.ShapeDtypeStruct((group, rows, 1), jnp.float32),
            jax.ShapeDtypeStruct((group * rows, HD), jnp.float32),
        )
    carried = list(carry) if carry is not None else []
    return pl.pallas_call(
        kernel,
        out_shape=out_shape,
        scratch_shapes=[pltpu.VMEM((block_count, group, rows, keys_per_block), jnp.float32)],
        compiler_params=pltpu.CompilerParams(vmem_limit_bytes=48 * 1024 * 1024),
        cost_estimate=cost,
    )(queries.reshape(group * rows, HD), low, high, live, key_index, *carried, *kv_blocks)


def attention(queries, low, high, live, key_index, kv_blocks, late_count):
    group, rows, _ = queries.shape
    early = len(kv_blocks) - late_count
    carry = attention_part(
        queries, low, high, live, key_index[late_count:], kv_blocks[late_count:], None, False
    )
    out = attention_part(
        queries, low, high, live, key_index[:late_count], kv_blocks[:late_count], carry, True
    )
    return out.reshape(group, rows, HD)


def segment_bounds(slot_index, page_counts, pad_counts):
    prompt_count = page_counts.shape[0]
    slot_counts = page_counts * PAGE
    slot_ends = running_total(slot_counts)
    segment_id = jnp.sum((slot_index[:, None] >= slot_ends[None, :]).astype(jnp.int32), axis=1)
    one_hot = (segment_id[:, None] == jnp.arange(prompt_count, dtype=jnp.int32)[None, :]).astype(
        jnp.int32
    )
    first_slot = jnp.sum(one_hot * (slot_ends - slot_counts)[None, :], axis=1)
    live_count = jnp.sum(one_hot * (slot_counts - pad_counts)[None, :], axis=1)
    return first_slot, live_count


def per_device(tokens, norm_gain, w_query, w_key, w_value, page_counts, pad_counts, page_table):
    row_count = tokens.shape[0]
    stream_total = row_count * lax.axis_size("req")
    longest_prompt = min(8 * row_count, stream_total // 2)
    reach_blocks = min(WINDOW, longest_prompt) // row_count
    block_start = lax.axis_index("req") * row_count
    slot_index = block_start + jnp.arange(row_count, dtype=jnp.int32)
    segment_id, position, is_live = token_meta(slot_index, page_counts, pad_counts)
    query_rot, key_rot, value_rows = project(tokens, norm_gain, w_query, w_key, w_value, position)
    kv_heads = key_rot.shape[1]
    group_size = query_rot.shape[1] // kv_heads
    head_total = kv_heads * group_size
    packed = jnp.concatenate([key_rot, value_rows], axis=-1)

    first_slot, live_count = segment_bounds(slot_index, page_counts, pad_counts)
    low = jnp.maximum(first_slot, slot_index - WINDOW + 1)[:, None]
    high = jnp.minimum(slot_index, first_slot + live_count - 1)[:, None]
    live_flag = is_live.astype(jnp.int32)[:, None]
    key_count = (reach_blocks + 1) * row_count
    key_index = block_start - reach_blocks * row_count + jnp.arange(key_count, dtype=jnp.int32)
    key_index = key_index.reshape(reach_blocks + 1, row_count)
    live_rows = jnp.where(is_live[:, None, None], packed, jnp.zeros((), jnp.bfloat16))
    page_total = row_count // PAGE
    page_rows = (
        live_rows.reshape(page_total, PAGE, kv_heads, 2 * HD)
        .transpose(0, 2, 1, 3)
        .reshape(page_total, kv_heads, PAGE * 2 * HD)
    )
    tp_count = lax.axis_size("tp")
    slots_here = page_total // tp_count
    local_table = page_table[0]
    slot_hits = (local_table[None, :] == jnp.arange(page_total, dtype=jnp.int32)[:, None]).astype(
        jnp.int32
    )
    page_order = jnp.sum(slot_hits * jnp.arange(page_total, dtype=jnp.int32)[None, :], axis=1)
    page_order = page_order.reshape(tp_count, slots_here).T
    outgoing = page_rows[page_order].reshape(slots_here, tp_count * kv_heads, PAGE * 2 * HD)
    cache = lax.all_to_all(outgoing, "tp", split_axis=1, concat_axis=1, tiled=True)
    owns = [
        jnp.concatenate([key_rot[:, kv_id].T, value_rows[:, kv_id].T], axis=0)
        for kv_id in range(kv_heads)
    ]
    first_shifts = list(range(1, reach_blocks // 2 + 1))
    early = [{shift: passed_along(own, "req", shift) for shift in first_shifts} for own in owns]
    held, cache = lax.optimization_barrier((owns, cache))
    per_kv = []
    for kv_id in range(kv_heads):
        own = held[kv_id]
        arrived = dict(early[kv_id])
        for shift in range(reach_blocks // 2 + 1, reach_blocks + 1):
            arrived[shift] = passed_along(own, "req", shift)
        blocks = [arrived[shift] for shift in range(reach_blocks, 0, -1)]
        head_queries = jnp.transpose(
            query_rot[:, kv_id * group_size:(kv_id + 1) * group_size], (1, 0, 2)
        )
        per_kv.append(
            attention(head_queries, low, high, live_flag, key_index, blocks + [own], 2)
        )
    context = jnp.transpose(jnp.concatenate(per_kv, axis=0), (1, 0, 2)).reshape(
        row_count, head_total * HD
    )
    return (context, cache)


def solution(mesh):
    in_specs = (
        P("req", None),
        P(),
        P(None, "tp"),
        P(None, "tp"),
        P(None, "tp"),
        P(),
        P(),
        P("req", None),
    )
    out_specs = (P("req", "tp"), P(("req", "tp"), None, None))
    return jax.shard_map(
        per_device, mesh=mesh, in_specs=in_specs, out_specs=out_specs, check_vma=False
    )
```

```python
import functools

import jax
import jax.numpy as jnp
from jax import lax
from jax.experimental import pallas as pl
from jax.experimental.pallas import tpu as pltpu
from jax.sharding import PartitionSpec as P

HD = 80
WINDOW = 4096
PAGE = 16


NORM_EPS = 1e-05
ROPE_BASE = 10000.0
MASKED_SCORE = -1e30


def passed_along(x, axis, by):
    size = lax.axis_size(axis)
    pairs = [(i, (i + by) % size) for i in range(size)]
    return lax.ppermute(x, axis, pairs)


def running_total(counts):
    order = jnp.arange(counts.shape[0], dtype=jnp.int32)
    upto = order[:, None] >= order[None, :]
    return jnp.sum(jnp.where(upto, counts[None, :], 0), axis=1)


def token_meta(slot_index, page_counts, pad_counts):
    prompt_count = page_counts.shape[0]
    slot_counts = page_counts * PAGE
    slot_ends = running_total(slot_counts)
    segment_id = jnp.sum((slot_index[:, None] >= slot_ends[None, :]).astype(jnp.int32), axis=1)
    one_hot = (segment_id[:, None] == jnp.arange(prompt_count, dtype=jnp.int32)[None, :]).astype(
        jnp.int32
    )
    first_slot = jnp.sum(one_hot * (slot_ends - slot_counts)[None, :], axis=1)
    live_count = jnp.sum(one_hot * (slot_counts - pad_counts)[None, :], axis=1)
    position = slot_index - first_slot
    inside = slot_index >= 0
    is_live = (position < live_count) & inside
    segment_id = jnp.where(inside, segment_id, -1)
    return (segment_id, position, is_live)


def rotate(vectors, position):
    half_width = vectors.shape[-1] // 2
    frequency = ROPE_BASE ** (-2.0 * jnp.arange(half_width, dtype=jnp.float32) / vectors.shape[-1])
    angles = position.astype(jnp.float32)[:, None, None] * frequency[None, None, :]
    cosine = jnp.cos(angles)
    sine_part = jnp.sin(angles)
    front_half = vectors[..., :half_width]
    back_half = vectors[..., half_width:]
    return jnp.concatenate(
        [front_half * cosine - back_half * sine_part, back_half * cosine + front_half * sine_part],
        axis=-1,
    )


def rotate_by_weights(normed, weights, position):
    head_count = weights.shape[1] // HD
    half_width = HD // 2
    split = weights.reshape(weights.shape[0], head_count, 2, half_width)
    swapped = jnp.concatenate([-split[:, :, 1:], split[:, :, :1]], axis=2).reshape(weights.shape)
    direct = jnp.dot(normed, weights, preferred_element_type=jnp.float32)
    partner = jnp.dot(normed, swapped, preferred_element_type=jnp.float32)
    frequency = ROPE_BASE ** (-2.0 * jnp.arange(half_width, dtype=jnp.float32) / HD)
    angles = position.astype(jnp.float32)[:, None] * frequency[None, :]
    cosine = jnp.tile(jnp.cos(angles), (1, 2 * head_count))
    sine_part = jnp.tile(jnp.sin(angles), (1, 2 * head_count))
    rotated = direct * cosine + partner * sine_part
    return rotated.reshape(normed.shape[0], head_count, HD).astype(jnp.bfloat16)


def project(tokens, norm_gain, w_query, w_key, w_value, position):
    row_count = tokens.shape[0]
    as_float = tokens.astype(jnp.float32)
    normed = (
        as_float
        * lax.rsqrt(jnp.mean(as_float * as_float, axis=-1, keepdims=True) + NORM_EPS)
        * norm_gain
    ).astype(jnp.bfloat16)
    query_rot = rotate_by_weights(normed, w_query, position)
    key_rot = jnp.dot(normed, w_key, preferred_element_type=jnp.float32).reshape(row_count, -1, HD)
    key_rot = rotate(key_rot, position).astype(jnp.bfloat16)
    value_rows = (
        jnp.dot(normed, w_value, preferred_element_type=jnp.float32)
        .reshape(row_count, -1, HD)
        .astype(jnp.bfloat16)
    )
    return (query_rot, key_rot, value_rows)


def attention_kernel(*refs, block_count, group, rows, carry_in, final):
    q_ref, lo_ref, hi_ref, live_ref, kidx_ref, need_ref = refs[:6]
    at = 6
    if carry_in:
        max_in_ref, total_in_ref, weighted_in_ref = refs[at:at + 3]
        at += 3
    kv_refs = refs[at:at + block_count]
    at += block_count
    out_refs = refs[at:-3]
    s_scr, total_scr, weighted_scr = refs[-3:]
    scale = HD ** (-0.5)
    queries = q_ref[...]
    low = lo_ref[...]
    high = hi_ref[...]
    row_max = jnp.full((group, rows, 1), MASKED_SCORE, jnp.float32)
    for b in range(block_count):
        keys = kv_refs[b][:HD, :]
        key_index = kidx_ref[b:b + 1, :]
        allowed = (key_index >= low) & (key_index <= high)
        tile = jnp.dot(queries, keys, preferred_element_type=jnp.float32).reshape(group, rows, -1)
        tile = jnp.where(allowed[None], tile * scale, MASKED_SCORE)
        s_scr[b] = tile
        row_max = jnp.maximum(row_max, jnp.max(tile, axis=-1, keepdims=True))
    if carry_in:
        earlier_max = max_in_ref[...]
        new_max = jnp.maximum(row_max, earlier_max)
        rescale = jnp.exp(earlier_max - new_max)
        total = total_in_ref[...] * rescale
        weighted = weighted_in_ref[...] * rescale.reshape(group * rows, 1)
        row_max = new_max
    else:
        total = jnp.zeros((group, rows, 1), jnp.float32)
        weighted = jnp.zeros((group * rows, HD), jnp.float32)
    total_scr[...] = total
    weighted_scr[...] = weighted
    for b in range(block_count):

        @pl.when(need_ref[b] != 0)
        def _(b=b):
            probs = jnp.exp(s_scr[b] - row_max)
            total_scr[...] += jnp.sum(probs, axis=-1, keepdims=True)
            weights = probs.astype(jnp.bfloat16).reshape(group * rows, -1)
            weighted_scr[...] += lax.dot_general(
                weights, kv_refs[b][HD:, :], (((1,), (1,)), ((), ())),
                preferred_element_type=jnp.float32,
            )

    total = total_scr[...]
    weighted = weighted_scr[...]
    if final:
        result = weighted.reshape(group, rows, HD) / total
        live = live_ref[...] != 0
        out_refs[0][...] = (
            jnp.where(live[None], result, 0.0).astype(out_refs[0].dtype).reshape(group * rows, HD)
        )
    else:
        out_refs[0][...] = row_max
        out_refs[1][...] = total
        out_refs[2][...] = weighted


def attention_part(queries, low, high, live, key_index, kv_blocks, carry, final):
    group, rows, _ = queries.shape
    block_count = len(kv_blocks)
    keys_per_block = kv_blocks[0].shape[1]
    kernel = functools.partial(
        attention_kernel, block_count=block_count, group=group, rows=rows,
        carry_in=carry is not None, final=final,
    )
    flops = 4 * group * rows * keys_per_block * block_count * HD
    cost = pl.CostEstimate(
        flops=flops,
        transcendentals=group * rows * keys_per_block * block_count,
        bytes_accessed=2 * (queries.size + sum(b.size for b in kv_blocks)) + 2 * queries.size,
    )
    if final:
        out_shape = jax.ShapeDtypeStruct((group * rows, HD), jnp.bfloat16)
    else:
        out_shape = (
            jax.ShapeDtypeStruct((group, rows, 1), jnp.float32),
            jax.ShapeDtypeStruct((group, rows, 1), jnp.float32),
            jax.ShapeDtypeStruct((group * rows, HD), jnp.float32),
        )
    carried = list(carry) if carry is not None else []
    valid = low <= high
    need = jnp.any(
        valid & (low <= key_index[:, -1][None, :]) & (high >= key_index[:, 0][None, :]), axis=0
    ).astype(jnp.int32)
    vmem = pl.BlockSpec(memory_space=pltpu.VMEM)
    in_specs = [vmem] * 5 + [pl.BlockSpec(memory_space=pltpu.SMEM)]
    in_specs += [vmem] * (len(carried) + block_count)
    return pl.pallas_call(
        kernel,
        out_shape=out_shape,
        in_specs=in_specs,
        scratch_shapes=[
            pltpu.VMEM((block_count, group, rows, keys_per_block), jnp.float32),
            pltpu.VMEM((group, rows, 1), jnp.float32),
            pltpu.VMEM((group * rows, HD), jnp.float32),
        ],
        compiler_params=pltpu.CompilerParams(vmem_limit_bytes=48 * 1024 * 1024),
        cost_estimate=cost,
    )(queries.reshape(group * rows, HD), low, high, live, key_index, need, *carried, *kv_blocks)


def attention(queries, low, high, live, key_index, kv_blocks, late_count):
    group, rows, _ = queries.shape
    early = len(kv_blocks) - late_count
    carry = attention_part(
        queries, low, high, live, key_index[late_count:], kv_blocks[late_count:], None, False
    )
    out = attention_part(
        queries, low, high, live, key_index[:late_count], kv_blocks[:late_count], carry, True
    )
    return out.reshape(group, rows, HD)


def segment_bounds(slot_index, page_counts, pad_counts):
    prompt_count = page_counts.shape[0]
    slot_counts = page_counts * PAGE
    slot_ends = running_total(slot_counts)
    segment_id = jnp.sum((slot_index[:, None] >= slot_ends[None, :]).astype(jnp.int32), axis=1)
    one_hot = (segment_id[:, None] == jnp.arange(prompt_count, dtype=jnp.int32)[None, :]).astype(
        jnp.int32
    )
    first_slot = jnp.sum(one_hot * (slot_ends - slot_counts)[None, :], axis=1)
    live_count = jnp.sum(one_hot * (slot_counts - pad_counts)[None, :], axis=1)
    return first_slot, live_count


def per_device(tokens, norm_gain, w_query, w_key, w_value, page_counts, pad_counts, page_table):
    row_count = tokens.shape[0]
    stream_total = row_count * lax.axis_size("req")
    longest_prompt = min(8 * row_count, stream_total // 2)
    reach_blocks = min(WINDOW, longest_prompt) // row_count
    block_start = lax.axis_index("req") * row_count
    slot_index = block_start + jnp.arange(row_count, dtype=jnp.int32)
    segment_id, position, is_live = token_meta(slot_index, page_counts, pad_counts)
    query_rot, key_rot, value_rows = project(tokens, norm_gain, w_query, w_key, w_value, position)
    kv_heads = key_rot.shape[1]
    group_size = query_rot.shape[1] // kv_heads
    head_total = kv_heads * group_size
    packed = jnp.concatenate([key_rot, value_rows], axis=-1)

    first_slot, live_count = segment_bounds(slot_index, page_counts, pad_counts)
    low = jnp.maximum(first_slot, slot_index - WINDOW + 1)[:, None]
    high = jnp.minimum(slot_index, first_slot + live_count - 1)[:, None]
    live_flag = is_live.astype(jnp.int32)[:, None]
    key_count = (reach_blocks + 1) * row_count
    key_index = block_start - reach_blocks * row_count + jnp.arange(key_count, dtype=jnp.int32)
    key_index = key_index.reshape(reach_blocks + 1, row_count)
    per_kv = []
    for kv_id in range(kv_heads):
        own = jnp.concatenate([key_rot[:, kv_id].T, value_rows[:, kv_id].T], axis=0)
        arrived = {shift: passed_along(own, "req", shift) for shift in range(1, reach_blocks + 1)}
        blocks = [arrived[shift] for shift in range(reach_blocks, 0, -1)]
        head_queries = jnp.transpose(
            query_rot[:, kv_id * group_size:(kv_id + 1) * group_size], (1, 0, 2)
        )
        per_kv.append(
            attention(head_queries, low, high, live_flag, key_index, blocks + [own], 2)
        )
    context = jnp.transpose(jnp.concatenate(per_kv, axis=0), (1, 0, 2)).reshape(
        row_count, head_total * HD
    )
    live_rows = jnp.where(is_live[:, None, None], packed, jnp.zeros((), jnp.bfloat16))
    page_total = row_count // PAGE
    page_rows = (
        live_rows.reshape(page_total, PAGE, kv_heads, 2 * HD)
        .transpose(0, 2, 1, 3)
        .reshape(page_total, kv_heads, PAGE * 2 * HD)
    )
    tp_count = lax.axis_size("tp")
    slots_here = page_total // tp_count
    local_table = page_table[0]
    slot_hits = (local_table[None, :] == jnp.arange(page_total, dtype=jnp.int32)[:, None]).astype(
        jnp.int32
    )
    page_order = jnp.sum(slot_hits * jnp.arange(page_total, dtype=jnp.int32)[None, :], axis=1)
    page_order = page_order.reshape(tp_count, slots_here).T
    outgoing = page_rows[page_order].reshape(slots_here, tp_count * kv_heads, PAGE * 2 * HD)
    cache = lax.all_to_all(outgoing, "tp", split_axis=1, concat_axis=1, tiled=True)
    return (context, cache)


def solution(mesh):
    in_specs = (
        P("req", None),
        P(),
        P(None, "tp"),
        P(None, "tp"),
        P(None, "tp"),
        P(),
        P(),
        P("req", None),
    )
    out_specs = (P("req", "tp"), P(("req", "tp"), None, None))
    return jax.shard_map(
        per_device, mesh=mesh, in_specs=in_specs, out_specs=out_specs, check_vma=False
    )
```

```python
import functools

import jax
import jax.numpy as jnp
from jax import lax
from jax.experimental import pallas as pl
from jax.experimental.pallas import tpu as pltpu
from jax.sharding import PartitionSpec as P

HD = 80
WINDOW = 4096
PAGE = 16


NORM_EPS = 1e-05
ROPE_BASE = 10000.0
MASKED_SCORE = -1e30


def passed_along(x, axis, by):
    size = lax.axis_size(axis)
    pairs = [(i, (i + by) % size) for i in range(size)]
    return lax.ppermute(x, axis, pairs)


def running_total(counts):
    order = jnp.arange(counts.shape[0], dtype=jnp.int32)
    upto = order[:, None] >= order[None, :]
    return jnp.sum(jnp.where(upto, counts[None, :], 0), axis=1)


def token_meta(slot_index, page_counts, pad_counts):
    prompt_count = page_counts.shape[0]
    slot_counts = page_counts * PAGE
    slot_ends = running_total(slot_counts)
    segment_id = jnp.sum((slot_index[:, None] >= slot_ends[None, :]).astype(jnp.int32), axis=1)
    one_hot = (segment_id[:, None] == jnp.arange(prompt_count, dtype=jnp.int32)[None, :]).astype(
        jnp.int32
    )
    first_slot = jnp.sum(one_hot * (slot_ends - slot_counts)[None, :], axis=1)
    live_count = jnp.sum(one_hot * (slot_counts - pad_counts)[None, :], axis=1)
    position = slot_index - first_slot
    inside = slot_index >= 0
    is_live = (position < live_count) & inside
    segment_id = jnp.where(inside, segment_id, -1)
    return (segment_id, position, is_live)


def rotate(vectors, position):
    half_width = vectors.shape[-1] // 2
    frequency = ROPE_BASE ** (-2.0 * jnp.arange(half_width, dtype=jnp.float32) / vectors.shape[-1])
    angles = position.astype(jnp.float32)[:, None, None] * frequency[None, None, :]
    cosine = jnp.cos(angles)
    sine_part = jnp.sin(angles)
    front_half = vectors[..., :half_width]
    back_half = vectors[..., half_width:]
    return jnp.concatenate(
        [front_half * cosine - back_half * sine_part, back_half * cosine + front_half * sine_part],
        axis=-1,
    )


def rotate_by_weights(normed, weights, position):
    head_count = weights.shape[1] // HD
    half_width = HD // 2
    split = weights.reshape(weights.shape[0], head_count, 2, half_width)
    swapped = jnp.concatenate([-split[:, :, 1:], split[:, :, :1]], axis=2).reshape(weights.shape)
    direct = jnp.dot(normed, weights, preferred_element_type=jnp.float32)
    partner = jnp.dot(normed, swapped, preferred_element_type=jnp.float32)
    frequency = ROPE_BASE ** (-2.0 * jnp.arange(half_width, dtype=jnp.float32) / HD)
    angles = position.astype(jnp.float32)[:, None] * frequency[None, :]
    cosine = jnp.tile(jnp.cos(angles), (1, 2 * head_count))
    sine_part = jnp.tile(jnp.sin(angles), (1, 2 * head_count))
    rotated = direct * cosine + partner * sine_part
    return rotated.reshape(normed.shape[0], head_count, HD).astype(jnp.bfloat16)


def project(tokens, norm_gain, w_query, w_key, w_value, position):
    row_count = tokens.shape[0]
    as_float = tokens.astype(jnp.float32)
    normed = (
        as_float
        * lax.rsqrt(jnp.mean(as_float * as_float, axis=-1, keepdims=True) + NORM_EPS)
        * norm_gain
    ).astype(jnp.bfloat16)
    query_rot = rotate_by_weights(normed, w_query, position)
    key_rot = jnp.dot(normed, w_key, preferred_element_type=jnp.float32).reshape(row_count, -1, HD)
    key_rot = rotate(key_rot, position).astype(jnp.bfloat16)
    value_rows = (
        jnp.dot(normed, w_value, preferred_element_type=jnp.float32)
        .reshape(row_count, -1, HD)
        .astype(jnp.bfloat16)
    )
    return (query_rot, key_rot, value_rows)


def attention_kernel(*refs, block_count, group, rows, carry_in, final):
    q_ref, lo_ref, hi_ref, live_ref, kidx_ref = refs[:5]
    at = 5
    if carry_in:
        max_in_ref, total_in_ref, weighted_in_ref = refs[at:at + 3]
        at += 3
    kv_refs = refs[at:at + block_count]
    at += block_count
    out_refs = refs[at:-1]
    s_scr = refs[-1]
    scale = HD ** (-0.5)
    queries = q_ref[...]
    low = lo_ref[...]
    high = hi_ref[...]
    row_max = jnp.full((group, rows, 1), MASKED_SCORE, jnp.float32)
    for b in range(block_count):
        keys = kv_refs[b][:HD, :]
        key_index = kidx_ref[b:b + 1, :]
        allowed = (key_index >= low) & (key_index <= high)
        tile = jnp.dot(queries, keys, preferred_element_type=jnp.float32).reshape(group, rows, -1)
        tile = jnp.where(allowed[None], tile * scale, MASKED_SCORE)
        s_scr[b] = tile
        row_max = jnp.maximum(row_max, jnp.max(tile, axis=-1, keepdims=True))
    if carry_in:
        earlier_max = max_in_ref[...]
        new_max = jnp.maximum(row_max, earlier_max)
        rescale = jnp.exp(earlier_max - new_max)
        total = total_in_ref[...] * rescale
        weighted = weighted_in_ref[...] * rescale.reshape(group * rows, 1)
        row_max = new_max
    else:
        total = jnp.zeros((group, rows, 1), jnp.float32)
        weighted = jnp.zeros((group * rows, HD), jnp.float32)
    for b in range(block_count):
        probs = jnp.exp(s_scr[b] - row_max)
        total = total + jnp.sum(probs, axis=-1, keepdims=True)
        weights = probs.astype(jnp.bfloat16).reshape(group * rows, -1)
        weighted = weighted + lax.dot_general(
            weights, kv_refs[b][HD:, :], (((1,), (1,)), ((), ())), preferred_element_type=jnp.float32
        )
    if final:
        result = weighted.reshape(group, rows, HD) / total
        live = live_ref[...] != 0
        out_refs[0][...] = (
            jnp.where(live[None], result, 0.0).astype(out_refs[0].dtype).reshape(group * rows, HD)
        )
    else:
        out_refs[0][...] = row_max
        out_refs[1][...] = total
        out_refs[2][...] = weighted


def attention_part(queries, low, high, live, key_index, kv_blocks, carry, final):
    group, rows, _ = queries.shape
    block_count = len(kv_blocks)
    keys_per_block = kv_blocks[0].shape[1]
    kernel = functools.partial(
        attention_kernel, block_count=block_count, group=group, rows=rows,
        carry_in=carry is not None, final=final,
    )
    flops = 4 * group * rows * keys_per_block * block_count * HD
    cost = pl.CostEstimate(
        flops=flops,
        transcendentals=group * rows * keys_per_block * block_count,
        bytes_accessed=2 * (queries.size + sum(b.size for b in kv_blocks)) + 2 * queries.size,
    )
    if final:
        out_shape = jax.ShapeDtypeStruct((group * rows, HD), jnp.bfloat16)
    else:
        out_shape = (
            jax.ShapeDtypeStruct((group, rows, 1), jnp.float32),
            jax.ShapeDtypeStruct((group, rows, 1), jnp.float32),
            jax.ShapeDtypeStruct((group * rows, HD), jnp.float32),
        )
    carried = list(carry) if carry is not None else []
    return pl.pallas_call(
        kernel,
        out_shape=out_shape,
        scratch_shapes=[pltpu.VMEM((block_count, group, rows, keys_per_block), jnp.float32)],
        compiler_params=pltpu.CompilerParams(vmem_limit_bytes=48 * 1024 * 1024),
        cost_estimate=cost,
    )(queries.reshape(group * rows, HD), low, high, live, key_index, *carried, *kv_blocks)


def attention(queries, low, high, live, key_index, kv_blocks, late_count):
    group, rows, _ = queries.shape
    early = len(kv_blocks) - late_count
    carry = attention_part(
        queries, low, high, live, key_index[late_count:], kv_blocks[late_count:], None, False
    )
    out = attention_part(
        queries, low, high, live, key_index[:late_count], kv_blocks[:late_count], carry, True
    )
    return out.reshape(group, rows, HD)


def segment_bounds(slot_index, page_counts, pad_counts):
    prompt_count = page_counts.shape[0]
    slot_counts = page_counts * PAGE
    slot_ends = running_total(slot_counts)
    segment_id = jnp.sum((slot_index[:, None] >= slot_ends[None, :]).astype(jnp.int32), axis=1)
    one_hot = (segment_id[:, None] == jnp.arange(prompt_count, dtype=jnp.int32)[None, :]).astype(
        jnp.int32
    )
    first_slot = jnp.sum(one_hot * (slot_ends - slot_counts)[None, :], axis=1)
    live_count = jnp.sum(one_hot * (slot_counts - pad_counts)[None, :], axis=1)
    return first_slot, live_count


def per_device(tokens, norm_gain, w_query, w_key, w_value, page_counts, pad_counts, page_table):
    row_count = tokens.shape[0]
    stream_total = row_count * lax.axis_size("req")
    longest_prompt = min(8 * row_count, stream_total // 2)
    reach_blocks = min(WINDOW, longest_prompt) // row_count
    block_start = lax.axis_index("req") * row_count
    slot_index = block_start + jnp.arange(row_count, dtype=jnp.int32)
    segment_id, position, is_live = token_meta(slot_index, page_counts, pad_counts)
    query_rot, key_rot, value_rows = project(tokens, norm_gain, w_query, w_key, w_value, position)
    kv_heads = key_rot.shape[1]
    group_size = query_rot.shape[1] // kv_heads
    head_total = kv_heads * group_size
    packed = jnp.concatenate([key_rot, value_rows], axis=-1)

    first_slot, live_count = segment_bounds(slot_index, page_counts, pad_counts)
    low = jnp.maximum(first_slot, slot_index - WINDOW + 1)[:, None]
    high = jnp.minimum(slot_index, first_slot + live_count - 1)[:, None]
    live_flag = is_live.astype(jnp.int32)[:, None]
    key_count = (reach_blocks + 1) * row_count
    key_index = block_start - reach_blocks * row_count + jnp.arange(key_count, dtype=jnp.int32)
    key_index = key_index.reshape(reach_blocks + 1, row_count)
    per_kv = []
    for kv_id in range(kv_heads):
        own = jnp.concatenate([key_rot[:, kv_id].T, value_rows[:, kv_id].T], axis=0)
        arrived = {shift: passed_along(own, "req", shift) for shift in range(1, reach_blocks + 1)}
        blocks = [arrived[shift] for shift in range(reach_blocks, 0, -1)]
        head_queries = jnp.transpose(
            query_rot[:, kv_id * group_size:(kv_id + 1) * group_size], (1, 0, 2)
        )
        per_kv.append(
            attention(head_queries, low, high, live_flag, key_index, blocks + [own], 4)
        )
    context = jnp.transpose(jnp.concatenate(per_kv, axis=0), (1, 0, 2)).reshape(
        row_count, head_total * HD
    )
    live_rows = jnp.where(is_live[:, None, None], packed, jnp.zeros((), jnp.bfloat16))
    page_total = row_count // PAGE
    page_rows = (
        live_rows.reshape(page_total, PAGE, kv_heads, 2 * HD)
        .transpose(0, 2, 1, 3)
        .reshape(page_total, kv_heads, PAGE * 2 * HD)
    )
    tp_count = lax.axis_size("tp")
    slots_here = page_total // tp_count
    local_table = page_table[0]
    slot_hits = (local_table[None, :] == jnp.arange(page_total, dtype=jnp.int32)[:, None]).astype(
        jnp.int32
    )
    page_order = jnp.sum(slot_hits * jnp.arange(page_total, dtype=jnp.int32)[None, :], axis=1)
    page_order = page_order.reshape(tp_count, slots_here).T
    outgoing = page_rows[page_order].reshape(slots_here, tp_count * kv_heads, PAGE * 2 * HD)
    cache = lax.all_to_all(outgoing, "tp", split_axis=1, concat_axis=1, tiled=True)
    return (context, cache)


def solution(mesh):
    in_specs = (
        P("req", None),
        P(),
        P(None, "tp"),
        P(None, "tp"),
        P(None, "tp"),
        P(),
        P(),
        P("req", None),
    )
    out_specs = (P("req", "tp"), P(("req", "tp"), None, None))
    return jax.shard_map(
        per_device, mesh=mesh, in_specs=in_specs, out_specs=out_specs, check_vma=False
    )
```
